32 devices in a mesh: dp: 8 (over z, core), tensor: 4 (over y, x).
Axes of the slice: x: 2, y: 2, z: 4, core: 2. Of those that a mesh axis runs over, the one named last changes fastest.
Arguments:
- context: bfloat16 [2048, 3072], P('dp', 'tensor'), may hold values from -6 to 6
- residual_in: bfloat16 [2048, 3072], P('dp', 'tensor'), may hold values from -6 to 6
- out_proj: bfloat16 [3072, 3072], P('tensor'), may hold values from -0.15625 to 0.15625
- members: int32 [2048, 1], P('dp'), may hold values from 0 to 7; in each aligned block of 256 rows (0 to 255, 256 to 511, ...) at most 40 rows name the same one
- host_group: int32 [8], replicated, may hold values from 0 to 7, each once
- member_proj: bfloat16 [8, 3072, 3072], P('dp', None, 'tensor'), may hold values from -0.15625 to 0.15625
- member_head: float32 [8, 3072], P('dp', 'tensor'), may hold values from -6 to 6
Outputs:
- generated: bfloat16 [2048, 3072], P('dp', 'tensor')
- input_grad: bfloat16 [2048, 3072], P('dp', 'tensor')
The draws below stay inside these ranges and needn't reach their ends.
Inputs may be any that keep to these rules, and one draw needn't show every extreme that they name: `members`: within the rows of one dp group (256 rows), no member index is named by more than 40 rows, and in every draw some index is named by exactly 40 rows of some group. `host_group`: each member is hosted by a different dp group.
All inputs are finite; a program needn't handle non-finite values.
Results may differ from the reference program's by a relative error of at most 0.02.
Values may be sent and summed in bfloat16 or wider, within the bound.
No kernel may reach another device: no remote copies, remote signals or barrier semaphores. Data moves between devices by JAX's collectives and lax.ppermute only.
A program may use at most 64 MiB of HBM per device.

```python
import math
from functools import partial
import jax
import jax.numpy as jnp
import numpy as np
from jax import lax

D = 3072
TOK_DEV = 256
TOKENS = 2048
MEMBERS = 8
CAP = 40
SLOTS = 320
N_DP = 8
N_TENSOR = 4


def with_spikes(values, stream_key, source, target, shards_of, factor):
    owner, partner = [(jnp.arange(values.shape[dim]) // (values.shape[dim] // shards_of)).reshape([-1 if axis == dim else 1 for axis in range(values.ndim)]) for dim in (source, target)]
    chosen = jax.random.permutation(stream_key, shards_of)[partner]
    strong = (owner == chosen) | (owner == (partner + shards_of // 2) % shards_of)
    return jnp.where(strong, factor * values, values)


def steps_of(own_key, shape, split, smallest, top_value):
    loudness = 1.0
    for axis_at, parts in split:
        draws = jax.random.uniform(jax.random.fold_in(jax.random.fold_in(own_key, 6), axis_at), (parts,), jnp.float32, smallest / len(split), top_value / len(split))
        loudness = loudness * jnp.repeat(jnp.exp(draws), shape[axis_at] // parts).reshape((-1,) + (1,) * (len(shape) - 1 - axis_at))
    return loudness


def routed_block(own_key, own, number, rows, number_of, top, bound, skew):
    sequence = jax.random.permutation(own_key, number_of)
    packed, common = shares(number_of, rows * top, bound, skew, True), shares(number_of, rows * top, bound, skew, False)
    places = jnp.arange(number_of)

    def named(lengths, turn):
        used = int((lengths > 0).sum())
        fixed = max(1, used // 4)
        passed = fixed + (places - fixed + turn * (used - fixed)) % max(1, number_of - fixed)
        return jnp.zeros((number_of,), jnp.int32).at[sequence[jnp.where(places < fixed, places, passed)]].set(jnp.asarray(lengths, jnp.int32))

    lengths = jnp.where(number % 4 == 0, named(packed, number // 4), named(common, number - number // 4 - 1))
    mixed = jax.random.permutation(jax.random.fold_in(own, 3), number_of)
    donor, taker = mixed[0:number_of // 2 * 2:2], mixed[1:number_of // 2 * 2:2]
    margin = jnp.minimum(lengths[donor] - 1, bound - lengths[taker]) // 2
    margin = jnp.where((donor == sequence[0]) | (taker == sequence[0]) | (lengths[taker] == 0), 0, jnp.maximum(margin, 0))
    passed = jax.random.randint(jax.random.fold_in(own, 4), (number_of // 2,), 0, 1 << 20) % (margin + 1)
    lengths = lengths.at[donor].add(-passed).at[taker].add(passed)
    items = jnp.searchsorted(jnp.cumsum(lengths), jnp.arange(rows * top), side="right").astype(jnp.int32)
    listing = items.reshape(top, rows).T
    listing = listing[jax.random.permutation(jax.random.fold_in(own, 1), rows)]
    turn = jax.random.randint(jax.random.fold_in(own, 2), (rows, 1), 0, top)
    return jnp.take_along_axis(listing, (jnp.arange(top)[None, :] + turn) % top, axis=1)


def shares(count, total, reach, slope, full):
    portions = [(1 << 20) // math.isqrt(grade ** slope) + 1 for grade in range(1, count + 1)]
    largest = reach if full else min(reach, max(-(-total // count), total * portions[0] // sum(portions)))
    least = 1 if total - largest >= count - 1 else 0
    holding, surplus = [largest] + [least] * (count - 1), total - largest - least * (count - 1)
    while surplus > 0:
        movable = [i for i in range(1, count) if holding[i] < largest] or [i for i in range(1, count) if holding[i] < reach]
        whole, left = sum([portions[i] for i in movable]), surplus
        for i in movable:
            more = min(reach - holding[i], max(1, left * portions[i] // whole), surplus)
            holding[i] = holding[i] + more
            surplus = surplus - more
    return np.array(holding)


def bell_draw(rng, shape, scale, limit, pieces=(), kind=jnp.bfloat16):
    loudness = steps_of(rng, shape, pieces, -0.22, 0.18) if pieces else 1.0
    array = jax.random.normal(rng, shape, jnp.float32) * scale * loudness
    return jnp.minimum(jnp.maximum(array, -limit), limit).astype(kind)


def noise_with(rng, extent, spread, bound, shards, heavy, held_as=jnp.bfloat16):
    array = spread * jax.random.normal(rng, extent, jnp.float32)
    if shards:
        array = array * steps_of(rng, extent, shards, -0.22, 0.18)
    return jnp.clip(with_spikes(array, jax.random.fold_in(rng, 3), *heavy), -bound, bound).astype(held_as)


def setup_inputs(seed: int = 0) -> dict:
    key_list = jax.random.split(jax.random.key(seed), 8)
    context = bell_draw(key_list[0], (TOKENS, D), 1.0, 6.0, ((0, 8), (1, 4)))
    residual_in = bell_draw(key_list[1], (TOKENS, D), 1.0, 6.0, ((0, 8), (1, 4)))
    out_proj = noise_with(key_list[2], (D, D), D ** -0.5, 0.15625, ((0, 4),), (0, 1, 4, 2.0))
    members_keys = jax.random.split(jax.random.fold_in(key_list[3], 1), TOKENS // TOK_DEV)
    members_turns = jax.random.permutation(jax.random.fold_in(key_list[3], 3), TOKENS // TOK_DEV)
    members = jax.vmap(lambda own, number: routed_block(jax.random.fold_in(key_list[3], 2), own, number, TOK_DEV, N_DP, 1, CAP, 1))(members_keys, members_turns).reshape((TOKENS, 1))
    host_group = jax.random.permutation(key_list[4], N_DP).astype(jnp.int32)
    member_proj = noise_with(key_list[5], (MEMBERS, D, D), D ** -0.5, 0.15625, ((0, 8), (2, 4)), (2, 1, 4, 2.0))
    member_head = bell_draw(key_list[6], (MEMBERS, D), 1.0, 6.0, ((0, 8), (1, 4)), jnp.float32)
    return {"context": context, "residual_in": residual_in, "out_proj": out_proj, "members": members, "host_group": host_group, "member_proj": member_proj, "member_head": member_head}


def slope_times(values, weights):
    _, back_fn = jax.vjp(partial(jax.nn.gelu, approximate=True), values)
    return back_fn(weights)[0]

def reference(context, residual_in, out_proj, members, host_group, member_proj, member_head):
    share = D // N_TENSOR
    running = residual_in.astype(jnp.float32)
    for tensor_group in range(N_TENSOR):
        first_col = tensor_group * share
        head_part = jnp.dot(context[:, first_col:first_col + share], out_proj[first_col:first_col + share, :], preferred_element_type=jnp.float32)
        head_part = lax.optimization_barrier(head_part.astype(jnp.bfloat16))
        running = running + head_part.astype(jnp.float32)
    generated = running.astype(jnp.bfloat16)
    destination = host_group[members[:, 0]].astype(jnp.int32)
    dest_grid = destination.reshape(N_DP, TOK_DEV)
    dest_hot = (dest_grid[:, :, None] == jnp.arange(N_DP, dtype=jnp.int32)[None, None, :]).astype(jnp.int32)
    rank_in = lax.optimization_barrier(jnp.sum((jnp.cumsum(dest_hot, axis=1) - dest_hot) * dest_hot, axis=2))
    source_group = jnp.repeat(jnp.arange(N_DP, dtype=jnp.int32), TOK_DEV)
    slot_of = (source_group * CAP + rank_in.reshape(-1)).astype(jnp.int32)
    critic_in = jnp.zeros((N_DP, SLOTS, D), generated.dtype).at[destination, slot_of].set(generated)

    def critic(member_index):
        rows_in = critic_in[member_index]
        projection = member_proj[member_index]
        pre_act = jnp.dot(rows_in, projection, preferred_element_type=jnp.float32)
        head_row = jnp.broadcast_to(member_head[member_index].astype(jnp.float32)[None, :], pre_act.shape)
        pre_grad = (-slope_times(pre_act, head_row)).astype(jnp.bfloat16)
        summed = jnp.zeros((SLOTS, D), jnp.float32)
        for tensor_group in range(N_TENSOR):
            first_col = tensor_group * share
            back_part = jnp.dot(pre_grad[:, first_col:first_col + share], projection[:, first_col:first_col + share].T, preferred_element_type=jnp.float32)
            back_part = lax.optimization_barrier(back_part.astype(jnp.bfloat16))
            summed = summed + back_part.astype(jnp.float32)
        return summed.astype(jnp.bfloat16)
    critic_grad = lax.map(critic, jnp.arange(N_DP, dtype=jnp.int32))
    input_grad = critic_grad[destination, slot_of]
    return (generated, input_grad)
```

```python
from functools import partial

import jax
import jax.numpy as jnp
from jax import lax
from jax.sharding import PartitionSpec as P


def slope_times(values, weights):
    _, back_fn = jax.vjp(partial(jax.nn.gelu, approximate=True), values)
    return back_fn(weights)[0]


def is_pow2(n):
    return n & (n - 1) == 0


def partner_of(me, s, n):
    return me ^ s if is_pow2(n) else (me + s) % n


def pairs_for(s, n):
    if is_pow2(n):
        return [(i, i ^ s) for i in range(n)]
    return [(i, (i + s) % n) for i in range(n)]


def sources_for(s, n):
    if is_pow2(n):
        return lambda me: me ^ s
    return lambda me: (me - s) % n


def reduce_blocks(blocks, axis):
    n = blocks.shape[0]
    me = lax.axis_index(axis)
    total = lax.dynamic_index_in_dim(blocks, me, 0, keepdims=False).astype(jnp.float32)
    for s in range(1, n):
        chunk = lax.dynamic_index_in_dim(blocks, partner_of(me, s, n), 0, keepdims=False)
        total = total + lax.ppermute(chunk, axis, pairs_for(s, n)).astype(jnp.float32)
    return total


def gather_blocks(x, axis):
    n = lax.axis_size(axis)
    me = lax.axis_index(axis)
    got = [x] + [lax.ppermute(x, axis, pairs_for(s, n)) for s in range(1, n)]
    stacked = jnp.stack(got)
    if is_pow2(n):
        order = lax.iota(jnp.int32, n) ^ me
    else:
        order = (me - lax.iota(jnp.int32, n)) % n
    return jnp.take(stacked, order, axis=0)


def swap_blocks(blocks, axis):
    n = blocks.shape[0]
    if n > 16:
        return lax.all_to_all(blocks, axis, 0, 0, tiled=True)
    me = lax.axis_index(axis)
    got = [lax.dynamic_index_in_dim(blocks, me, 0, keepdims=False)]
    for s in range(1, n):
        chunk = lax.dynamic_index_in_dim(blocks, partner_of(me, s, n), 0, keepdims=False)
        got.append(lax.ppermute(chunk, axis, pairs_for(s, n)))
    stacked = jnp.stack(got)
    if is_pow2(n):
        order = lax.iota(jnp.int32, n) ^ me
    else:
        order = (me - lax.iota(jnp.int32, n)) % n
    return jnp.take(stacked, order, axis=0)


def shards(context, residual_in, out_proj, members, host_group, member_proj, member_head):
    tok_rows, width = context.shape
    group_count = lax.axis_size("dp")
    tensor_count = lax.axis_size("tensor")
    capacity = max(2, (5 * tok_rows + 4 * group_count - 1) // (4 * group_count))
    slot_count = group_count * capacity
    projection = member_proj[0]

    head_blocks = jnp.einsum(
        "rc,ckd->krd",
        context,
        out_proj.reshape(width, tensor_count, width),
        preferred_element_type=jnp.float32,
    ).astype(jnp.bfloat16)
    summed = reduce_blocks(head_blocks, "tensor")
    generated = (summed + residual_in.astype(jnp.float32)).astype(jnp.bfloat16)

    group_ids = lax.iota(jnp.int32, group_count)
    member_ids = members[:, 0]
    destination = jnp.sum(
        jnp.where(member_ids[:, None] == group_ids[None, :], host_group[None, :], 0), axis=1
    )
    dest_hot = (destination[:, None] == group_ids[None, :]).astype(jnp.int32)
    earlier = jnp.cumsum(dest_hot, axis=0) - dest_hot
    rank_in = jnp.sum(earlier * dest_hot, axis=1)
    slot_of = destination * capacity + rank_in
    placing = (slot_of[:, None] == lax.iota(jnp.int32, slot_count)[None, :]).astype(jnp.bfloat16)

    outgoing = lax.dot_general(
        placing, generated, (((0,), (0,)), ((), ())), preferred_element_type=jnp.float32
    ).astype(jnp.bfloat16)
    arrived = swap_blocks(outgoing.reshape(group_count, capacity, width), "dp")
    arrived = arrived.reshape(slot_count, width)
    gathered = gather_blocks(arrived, "tensor")
    pre_act = jnp.einsum(
        "ksd,kdo->so",
        gathered,
        projection.reshape(tensor_count, width, width),
        preferred_element_type=jnp.float32,
    )
    head_row = jnp.broadcast_to(member_head[0][None, :], pre_act.shape)
    pre_grad = (-slope_times(pre_act, head_row)).astype(jnp.bfloat16)
    back_blocks = jnp.einsum(
        "so,kdo->ksd",
        pre_grad,
        projection.reshape(tensor_count, width, width),
        preferred_element_type=jnp.float32,
    ).astype(jnp.bfloat16)
    critic_grad = reduce_blocks(back_blocks, "tensor").astype(jnp.bfloat16)
    returned = swap_blocks(critic_grad.reshape(group_count, capacity, width), "dp")
    returned = returned.reshape(slot_count, width)
    input_grad = jnp.dot(placing, returned, preferred_element_type=jnp.float32).astype(jnp.bfloat16)
    return (generated, input_grad)


def solution(mesh):
    in_specs = (
        P("dp", "tensor"),
        P("dp", "tensor"),
        P("tensor", None),
        P("dp", None),
        P(),
        P("dp", None, "tensor"),
        P("dp", "tensor"),
    )
    out_specs = (P("dp", "tensor"), P("dp", "tensor"))
    return jax.shard_map(shards, mesh=mesh, in_specs=in_specs, out_specs=out_specs, check_vma=False)
```

```python
from functools import partial

import jax
import jax.numpy as jnp
from jax import lax
from jax.sharding import PartitionSpec as P


def slope_times(values, weights):
    _, back_fn = jax.vjp(partial(jax.nn.gelu, approximate=True), values)
    return back_fn(weights)[0]


def is_pow2(n):
    return n & (n - 1) == 0


def partner_of(me, s, n):
    return me ^ s if is_pow2(n) else (me + s) % n


def pairs_for(s, n):
    if is_pow2(n):
        return [(i, i ^ s) for i in range(n)]
    return [(i, (i + s) % n) for i in range(n)]


def sources_for(s, n):
    if is_pow2(n):
        return lambda me: me ^ s
    return lambda me: (me - s) % n


def reduce_blocks(blocks, axis):
    n = blocks.shape[0]
    me = lax.axis_index(axis)
    total = lax.dynamic_index_in_dim(blocks, me, 0, keepdims=False).astype(jnp.float32)
    for s in range(1, n):
        chunk = lax.dynamic_index_in_dim(blocks, partner_of(me, s, n), 0, keepdims=False)
        total = total + lax.ppermute(chunk, axis, pairs_for(s, n)).astype(jnp.float32)
    return total


def gather_blocks(x, axis):
    n = lax.axis_size(axis)
    me = lax.axis_index(axis)
    got = [x] + [lax.ppermute(x, axis, pairs_for(s, n)) for s in range(1, n)]
    stacked = jnp.stack(got)
    if is_pow2(n):
        order = lax.iota(jnp.int32, n) ^ me
    else:
        order = (me - lax.iota(jnp.int32, n)) % n
    return jnp.take(stacked, order, axis=0)


def swap_blocks(blocks, axis):
    n = blocks.shape[0]
    if n > 16:
        return lax.all_to_all(blocks, axis, 0, 0, tiled=True)
    me = lax.axis_index(axis)
    got = [lax.dynamic_index_in_dim(blocks, me, 0, keepdims=False)]
    for s in range(1, n):
        chunk = lax.dynamic_index_in_dim(blocks, partner_of(me, s, n), 0, keepdims=False)
        got.append(lax.ppermute(chunk, axis, pairs_for(s, n)))
    stacked = jnp.stack(got)
    if is_pow2(n):
        order = lax.iota(jnp.int32, n) ^ me
    else:
        order = (me - lax.iota(jnp.int32, n)) % n
    return jnp.take(stacked, order, axis=0)


SLOT_CHUNKS = 1


def shards(context, residual_in, out_proj, members, host_group, member_proj, member_head):
    tok_rows, width = context.shape
    group_count = lax.axis_size("dp")
    tensor_count = lax.axis_size("tensor")
    capacity = max(2, (5 * tok_rows + 4 * group_count - 1) // (4 * group_count))
    chunks = SLOT_CHUNKS if capacity % SLOT_CHUNKS == 0 else 1
    chunk_cap = capacity // chunks
    chunk_slots = group_count * chunk_cap
    me_t = lax.axis_index("tensor")
    partners = [partner_of(me_t, s, tensor_count) for s in range(tensor_count)]
    projection = member_proj[0]
    proj_blocks = projection.reshape(tensor_count, width, projection.shape[1])
    proj_parts = [lax.dynamic_index_in_dim(proj_blocks, p, 0, keepdims=False) for p in partners]

    head_terms = jnp.dot(context, out_proj, preferred_element_type=jnp.float32).astype(jnp.bfloat16)
    head_blocks = head_terms.reshape(tok_rows, tensor_count, width)
    summed = lax.dynamic_index_in_dim(head_blocks, me_t, 1, keepdims=False).astype(jnp.float32)
    summed = summed + residual_in.astype(jnp.float32)
    for s in range(1, tensor_count):
        chunk = lax.dynamic_index_in_dim(head_blocks, partners[s], 1, keepdims=False)
        summed = summed + lax.ppermute(chunk, "tensor", pairs_for(s, tensor_count)).astype(jnp.float32)
    generated = summed.astype(jnp.bfloat16)

    group_ids = lax.iota(jnp.int32, group_count)
    member_ids = members[:, 0]
    destination = jnp.sum(
        jnp.where(member_ids[:, None] == group_ids[None, :], host_group[None, :], 0), axis=1
    )
    dest_hot = (destination[:, None] == group_ids[None, :]).astype(jnp.int32)
    earlier = jnp.cumsum(dest_hot, axis=0) - dest_hot
    rank_in = jnp.sum(earlier * dest_hot, axis=1)
    slot_ids = lax.iota(jnp.int32, chunk_slots)
    head_row = member_head[0][None, :]

    input_grad = None
    for c in range(chunks):
        local_rank = rank_in - c * chunk_cap
        inside = (local_rank >= 0) & (local_rank < chunk_cap)
        slot_of = destination * chunk_cap + local_rank
        placing = ((slot_of[:, None] == slot_ids[None, :]) & inside[:, None]).astype(jnp.bfloat16)
        outgoing = lax.dot_general(
            placing, generated, (((0,), (0,)), ((), ())), preferred_element_type=jnp.float32
        ).astype(jnp.bfloat16)
        arrived = swap_blocks(outgoing.reshape(group_count, chunk_cap, width), "dp")
        arrived = arrived.reshape(chunk_slots, width)
        pre_act = jnp.dot(arrived, proj_parts[0], preferred_element_type=jnp.float32)
        for s in range(1, tensor_count):
            got = lax.ppermute(arrived, "tensor", pairs_for(s, tensor_count))
            pre_act = pre_act + jnp.dot(got, proj_parts[s], preferred_element_type=jnp.float32)
        pre_grad = (-slope_times(pre_act, jnp.broadcast_to(head_row, pre_act.shape))).astype(jnp.bfloat16)
        back = [
            lax.dot_general(
                pre_grad, part, (((1,), (1,)), ((), ())), preferred_element_type=jnp.float32
            ).astype(jnp.bfloat16)
            for part in proj_parts
        ]
        critic_grad = back[0].astype(jnp.float32)
        for s in range(1, tensor_count):
            critic_grad = critic_grad + lax.ppermute(
                back[s], "tensor", pairs_for(s, tensor_count)
            ).astype(jnp.float32)
        critic_grad = critic_grad.astype(jnp.bfloat16)
        returned = swap_blocks(critic_grad.reshape(group_count, chunk_cap, width), "dp")
        returned = returned.reshape(chunk_slots, width)
        part = jnp.dot(placing, returned, preferred_element_type=jnp.float32)
        input_grad = part if input_grad is None else input_grad + part
    return (generated, input_grad.astype(jnp.bfloat16))


def solution(mesh):
    in_specs = (
        P("dp", "tensor"),
        P("dp", "tensor"),
        P("tensor", None),
        P("dp", None),
        P(),
        P("dp", None, "tensor"),
        P("dp", "tensor"),
    )
    out_specs = (P("dp", "tensor"), P("dp", "tensor"))
    return jax.shard_map(shards, mesh=mesh, in_specs=in_specs, out_specs=out_specs, check_vma=False)
```

```python
from functools import partial

import jax
import jax.numpy as jnp
from jax import lax
from jax.sharding import PartitionSpec as P


def slope_times(values, weights):
    _, back_fn = jax.vjp(partial(jax.nn.gelu, approximate=True), values)
    return back_fn(weights)[0]


def is_pow2(n):
    return n & (n - 1) == 0


def partner_of(me, s, n):
    return me ^ s if is_pow2(n) else (me + s) % n


def pairs_for(s, n):
    if is_pow2(n):
        return [(i, i ^ s) for i in range(n)]
    return [(i, (i + s) % n) for i in range(n)]


def sources_for(s, n):
    if is_pow2(n):
        return lambda me: me ^ s
    return lambda me: (me - s) % n


def reduce_blocks(blocks, axis):
    n = blocks.shape[0]
    me = lax.axis_index(axis)
    total = lax.dynamic_index_in_dim(blocks, me, 0, keepdims=False).astype(jnp.float32)
    for s in range(1, n):
        chunk = lax.dynamic_index_in_dim(blocks, partner_of(me, s, n), 0, keepdims=False)
        total = total + lax.ppermute(chunk, axis, pairs_for(s, n)).astype(jnp.float32)
    return total


def gather_blocks(x, axis):
    n = lax.axis_size(axis)
    me = lax.axis_index(axis)
    got = [x] + [lax.ppermute(x, axis, pairs_for(s, n)) for s in range(1, n)]
    stacked = jnp.stack(got)
    if is_pow2(n):
        order = lax.iota(jnp.int32, n) ^ me
    else:
        order = (me - lax.iota(jnp.int32, n)) % n
    return jnp.take(stacked, order, axis=0)


def swap_blocks(blocks, axis):
    n = blocks.shape[0]
    if n > 16:
        return lax.all_to_all(blocks, axis, 0, 0, tiled=True)
    me = lax.axis_index(axis)
    got = [lax.dynamic_index_in_dim(blocks, me, 0, keepdims=False)]
    for s in range(1, n):
        chunk = lax.dynamic_index_in_dim(blocks, partner_of(me, s, n), 0, keepdims=False)
        got.append(lax.ppermute(chunk, axis, pairs_for(s, n)))
    stacked = jnp.stack(got)
    if is_pow2(n):
        order = lax.iota(jnp.int32, n) ^ me
    else:
        order = (me - lax.iota(jnp.int32, n)) % n
    return jnp.take(stacked, order, axis=0)


SLOT_CHUNKS = 2


def shards(context, residual_in, out_proj, members, host_group, member_proj, member_head):
    tok_rows, width = context.shape
    group_count = lax.axis_size("dp")
    tensor_count = lax.axis_size("tensor")
    capacity = max(2, (5 * tok_rows + 4 * group_count - 1) // (4 * group_count))
    chunks = SLOT_CHUNKS if capacity % SLOT_CHUNKS == 0 else 1
    chunk_cap = capacity // chunks
    chunk_slots = group_count * chunk_cap
    me_t = lax.axis_index("tensor")
    partners = [partner_of(me_t, s, tensor_count) for s in range(tensor_count)]
    projection = member_proj[0]
    proj_blocks = projection.reshape(tensor_count, width, projection.shape[1])
    proj_parts = [lax.dynamic_index_in_dim(proj_blocks, p, 0, keepdims=False) for p in partners]

    head_terms = jnp.dot(context, out_proj, preferred_element_type=jnp.float32).astype(jnp.bfloat16)
    head_blocks = head_terms.reshape(tok_rows, tensor_count, width)
    summed = lax.dynamic_index_in_dim(head_blocks, me_t, 1, keepdims=False).astype(jnp.float32)
    summed = summed + residual_in.astype(jnp.float32)
    for s in range(1, tensor_count):
        chunk = lax.dynamic_index_in_dim(head_blocks, partners[s], 1, keepdims=False)
        summed = summed + lax.ppermute(chunk, "tensor", pairs_for(s, tensor_count)).astype(jnp.float32)
    generated = summed.astype(jnp.bfloat16)

    group_ids = lax.iota(jnp.int32, group_count)
    member_ids = members[:, 0]
    destination = jnp.sum(
        jnp.where(member_ids[:, None] == group_ids[None, :], host_group[None, :], 0), axis=1
    )
    dest_hot = (destination[:, None] == group_ids[None, :]).astype(jnp.int32)
    earlier = jnp.cumsum(dest_hot, axis=0) - dest_hot
    rank_in = jnp.sum(earlier * dest_hot, axis=1)
    slot_ids = lax.iota(jnp.int32, chunk_slots)
    head_row = member_head[0][None, :]

    input_grad = None
    for c in range(chunks):
        local_rank = rank_in - c * chunk_cap
        inside = (local_rank >= 0) & (local_rank < chunk_cap)
        slot_of = destination * chunk_cap + local_rank
        placing = ((slot_of[:, None] == slot_ids[None, :]) & inside[:, None]).astype(jnp.bfloat16)
        outgoing = lax.dot_general(
            placing, generated, (((0,), (0,)), ((), ())), preferred_element_type=jnp.float32
        ).astype(jnp.bfloat16)
        arrived = swap_blocks(outgoing.reshape(group_count, chunk_cap, width), "dp")
        arrived = arrived.reshape(chunk_slots, width)
        pre_act = jnp.dot(arrived, proj_parts[0], preferred_element_type=jnp.float32)
        for s in range(1, tensor_count):
            got = lax.ppermute(arrived, "tensor", pairs_for(s, tensor_count))
            pre_act = pre_act + jnp.dot(got, proj_parts[s], preferred_element_type=jnp.float32)
        pre_grad = (-slope_times(pre_act, jnp.broadcast_to(head_row, pre_act.shape))).astype(jnp.bfloat16)
        back = [
            lax.dot_general(
                pre_grad, part, (((1,), (1,)), ((), ())), preferred_element_type=jnp.float32
            ).astype(jnp.bfloat16)
            for part in proj_parts
        ]
        critic_grad = back[0].astype(jnp.float32)
        for s in range(1, tensor_count):
            critic_grad = critic_grad + lax.ppermute(
                back[s], "tensor", pairs_for(s, tensor_count)
            ).astype(jnp.float32)
        critic_grad = critic_grad.astype(jnp.bfloat16)
        returned = swap_blocks(critic_grad.reshape(group_count, chunk_cap, width), "dp")
        returned = returned.reshape(chunk_slots, width)
        part = jnp.dot(placing, returned, preferred_element_type=jnp.float32)
        input_grad = part if input_grad is None else input_grad + part
    return (generated, input_grad.astype(jnp.bfloat16))


def solution(mesh):
    in_specs = (
        P("dp", "tensor"),
        P("dp", "tensor"),
        P("tensor", None),
        P("dp", None),
        P(),
        P("dp", None, "tensor"),
        P("dp", "tensor"),
    )
    out_specs = (P("dp", "tensor"), P("dp", "tensor"))
    return jax.shard_map(shards, mesh=mesh, in_specs=in_specs, out_specs=out_specs, check_vma=False)
```

```python
from functools import partial

import jax
import jax.numpy as jnp
from jax import lax
from jax.sharding import PartitionSpec as P


def slope_times(values, weights):
    _, back_fn = jax.vjp(partial(jax.nn.gelu, approximate=True), values)
    return back_fn(weights)[0]


def is_pow2(n):
    return n & (n - 1) == 0


def partner_of(me, s, n):
    return me ^ s if is_pow2(n) else (me + s) % n


def pairs_for(s, n):
    if is_pow2(n):
        return [(i, i ^ s) for i in range(n)]
    return [(i, (i + s) % n) for i in range(n)]


def sources_for(s, n):
    if is_pow2(n):
        return lambda me: me ^ s
    return lambda me: (me - s) % n


def reduce_blocks(blocks, axis):
    n = blocks.shape[0]
    me = lax.axis_index(axis)
    total = lax.dynamic_index_in_dim(blocks, me, 0, keepdims=False).astype(jnp.float32)
    for s in range(1, n):
        chunk = lax.dynamic_index_in_dim(blocks, partner_of(me, s, n), 0, keepdims=False)
        total = total + lax.ppermute(chunk, axis, pairs_for(s, n)).astype(jnp.float32)
    return total


def gather_blocks(x, axis):
    n = lax.axis_size(axis)
    me = lax.axis_index(axis)
    got = [x] + [lax.ppermute(x, axis, pairs_for(s, n)) for s in range(1, n)]
    stacked = jnp.stack(got)
    if is_pow2(n):
        order = lax.iota(jnp.int32, n) ^ me
    else:
        order = (me - lax.iota(jnp.int32, n)) % n
    return jnp.take(stacked, order, axis=0)


def swap_blocks(blocks, axis):
    n = blocks.shape[0]
    if n > 16:
        return lax.all_to_all(blocks, axis, 0, 0, tiled=True)
    me = lax.axis_index(axis)
    got = [lax.dynamic_index_in_dim(blocks, me, 0, keepdims=False)]
    for s in range(1, n):
        chunk = lax.dynamic_index_in_dim(blocks, partner_of(me, s, n), 0, keepdims=False)
        got.append(lax.ppermute(chunk, axis, pairs_for(s, n)))
    stacked = jnp.stack(got)
    if is_pow2(n):
        order = lax.iota(jnp.int32, n) ^ me
    else:
        order = (me - lax.iota(jnp.int32, n)) % n
    return jnp.take(stacked, order, axis=0)


SLOT_CHUNKS = 1


def shards(context, residual_in, out_proj, members, host_group, member_proj, member_head):
    tok_rows, width = context.shape
    group_count = lax.axis_size("dp")
    tensor_count = lax.axis_size("tensor")
    capacity = max(2, (5 * tok_rows + 4 * group_count - 1) // (4 * group_count))
    chunks = SLOT_CHUNKS if capacity % SLOT_CHUNKS == 0 else 1
    chunk_cap = capacity // chunks
    chunk_slots = group_count * chunk_cap
    me_t = lax.axis_index("tensor")
    partners = [partner_of(me_t, s, tensor_count) for s in range(tensor_count)]
    projection = member_proj[0]
    proj_blocks = projection.reshape(tensor_count, width, projection.shape[1])
    proj_parts = [lax.dynamic_index_in_dim(proj_blocks, p, 0, keepdims=False) for p in partners]

    def head_term(p):
        columns = lax.dynamic_slice_in_dim(out_proj, p * width, width, axis=1)
        return jnp.dot(context, columns, preferred_element_type=jnp.float32).astype(jnp.bfloat16)

    received = [
        lax.ppermute(head_term(partners[s]), "tensor", pairs_for(s, tensor_count))
        for s in range(1, tensor_count)
    ]
    summed = head_term(me_t).astype(jnp.float32) + residual_in.astype(jnp.float32)
    for got in received:
        summed = summed + got.astype(jnp.float32)
    generated = summed.astype(jnp.bfloat16)

    group_ids = lax.iota(jnp.int32, group_count)
    member_ids = members[:, 0]
    destination = jnp.sum(
        jnp.where(member_ids[:, None] == group_ids[None, :], host_group[None, :], 0), axis=1
    )
    dest_hot = (destination[:, None] == group_ids[None, :]).astype(jnp.int32)
    earlier = jnp.cumsum(dest_hot, axis=0) - dest_hot
    rank_in = jnp.sum(earlier * dest_hot, axis=1)
    slot_ids = lax.iota(jnp.int32, chunk_slots)
    head_row = member_head[0][None, :]

    input_grad = None
    for c in range(chunks):
        local_rank = rank_in - c * chunk_cap
        inside = (local_rank >= 0) & (local_rank < chunk_cap)
        slot_of = destination * chunk_cap + local_rank
        placing = ((slot_of[:, None] == slot_ids[None, :]) & inside[:, None]).astype(jnp.bfloat16)
        outgoing = lax.dot_general(
            placing, generated, (((0,), (0,)), ((), ())), preferred_element_type=jnp.float32
        ).astype(jnp.bfloat16)
        arrived = swap_blocks(outgoing.reshape(group_count, chunk_cap, width), "dp")
        arrived = arrived.reshape(chunk_slots, width)
        pre_act = jnp.dot(arrived, proj_parts[0], preferred_element_type=jnp.float32)
        for s in range(1, tensor_count):
            got = lax.ppermute(arrived, "tensor", pairs_for(s, tensor_count))
            pre_act = pre_act + jnp.dot(got, proj_parts[s], preferred_element_type=jnp.float32)
        pre_grad = (-slope_times(pre_act, jnp.broadcast_to(head_row, pre_act.shape))).astype(jnp.bfloat16)
        back = [
            lax.dot_general(
                pre_grad, part, (((1,), (1,)), ((), ())), preferred_element_type=jnp.float32
            ).astype(jnp.bfloat16)
            for part in proj_parts
        ]
        critic_grad = back[0].astype(jnp.float32)
        for s in range(1, tensor_count):
            critic_grad = critic_grad + lax.ppermute(
                back[s], "tensor", pairs_for(s, tensor_count)
            ).astype(jnp.float32)
        critic_grad = critic_grad.astype(jnp.bfloat16)
        returned = swap_blocks(critic_grad.reshape(group_count, chunk_cap, width), "dp")
        returned = returned.reshape(chunk_slots, width)
        part = jnp.dot(placing, returned, preferred_element_type=jnp.float32)
        input_grad = part if input_grad is None else input_grad + part
    return (generated, input_grad.astype(jnp.bfloat16))


def solution(mesh):
    in_specs = (
        P("dp", "tensor"),
        P("dp", "tensor"),
        P("tensor", None),
        P("dp", None),
        P(),
        P("dp", None, "tensor"),
        P("dp", "tensor"),
    )
    out_specs = (P("dp", "tensor"), P("dp", "tensor"))
    return jax.shard_map(shards, mesh=mesh, in_specs=in_specs, out_specs=out_specs, check_vma=False)
```

```python
from functools import partial

import jax
import jax.numpy as jnp
from jax import lax
from jax.sharding import PartitionSpec as P


def slope_times(values, weights):
    _, back_fn = jax.vjp(partial(jax.nn.gelu, approximate=True), values)
    return back_fn(weights)[0]


def is_pow2(n):
    return n & (n - 1) == 0


def partner_of(me, s, n):
    return me ^ s if is_pow2(n) else (me + s) % n


def pairs_for(s, n):
    if is_pow2(n):
        return [(i, i ^ s) for i in range(n)]
    return [(i, (i + s) % n) for i in range(n)]


def sources_for(s, n):
    if is_pow2(n):
        return lambda me: me ^ s
    return lambda me: (me - s) % n


def reduce_blocks(blocks, axis):
    n = blocks.shape[0]
    me = lax.axis_index(axis)
    total = lax.dynamic_index_in_dim(blocks, me, 0, keepdims=False).astype(jnp.float32)
    for s in range(1, n):
        chunk = lax.dynamic_index_in_dim(blocks, partner_of(me, s, n), 0, keepdims=False)
        total = total + lax.ppermute(chunk, axis, pairs_for(s, n)).astype(jnp.float32)
    return total


def gather_blocks(x, axis):
    n = lax.axis_size(axis)
    me = lax.axis_index(axis)
    got = [x] + [lax.ppermute(x, axis, pairs_for(s, n)) for s in range(1, n)]
    stacked = jnp.stack(got)
    if is_pow2(n):
        order = lax.iota(jnp.int32, n) ^ me
    else:
        order = (me - lax.iota(jnp.int32, n)) % n
    return jnp.take(stacked, order, axis=0)


def swap_blocks(blocks, axis):
    n = blocks.shape[0]
    if n > 16:
        return lax.all_to_all(blocks, axis, 0, 0, tiled=True)
    me = lax.axis_index(axis)
    got = [lax.dynamic_index_in_dim(blocks, me, 0, keepdims=False)]
    for s in range(1, n):
        chunk = lax.dynamic_index_in_dim(blocks, partner_of(me, s, n), 0, keepdims=False)
        got.append(lax.ppermute(chunk, axis, pairs_for(s, n)))
    stacked = jnp.stack(got)
    if is_pow2(n):
        order = lax.iota(jnp.int32, n) ^ me
    else:
        order = (me - lax.iota(jnp.int32, n)) % n
    return jnp.take(stacked, order, axis=0)


def bit_orders(n):
    bits = [1 << i for i in range(n.bit_length() - 1)]
    return [bits, bits[::-1]]


def reduce_scatter_tree(block_fn, axis, n):
    outs = []
    for h, order in enumerate(bit_orders(n)):
        held = {d: block_fn(d, h) for d in range(n)}
        for bit in order:
            send = sorted(d for d in held if d & bit)
            keep = sorted(d for d in held if not d & bit)
            payload = jnp.concatenate([held[d].astype(jnp.bfloat16) for d in send], axis=0)
            got = lax.ppermute(payload, axis, [(i, i ^ bit) for i in range(n)])
            rows = held[keep[0]].shape[0]
            held = {
                d: held[d].astype(jnp.float32) + got[i * rows:(i + 1) * rows].astype(jnp.float32)
                for i, d in enumerate(keep)
            }
        outs.append(held[0])
    return outs


def all_gather_tree(halves, axis, n):
    outs = []
    for h, order in enumerate(bit_orders(n)):
        held = {0: halves[h]}
        for bit in order:
            have = sorted(held)
            payload = jnp.concatenate([held[d] for d in have], axis=0)
            got = lax.ppermute(payload, axis, [(i, i ^ bit) for i in range(n)])
            rows = halves[h].shape[0]
            for i, d in enumerate(have):
                held[d ^ bit] = got[i * rows:(i + 1) * rows]
        outs.append(held)
    return outs


SLOT_CHUNKS = 1


def shards(context, residual_in, out_proj, members, host_group, member_proj, member_head):
    tok_rows, width = context.shape
    group_count = lax.axis_size("dp")
    tensor_count = lax.axis_size("tensor")
    capacity = max(2, (5 * tok_rows + 4 * group_count - 1) // (4 * group_count))
    chunks = SLOT_CHUNKS if capacity % SLOT_CHUNKS == 0 else 1
    chunk_cap = capacity // chunks
    chunk_slots = group_count * chunk_cap
    me_t = lax.axis_index("tensor")
    partners = [partner_of(me_t, s, tensor_count) for s in range(tensor_count)]
    projection = member_proj[0]
    proj_blocks = projection.reshape(tensor_count, width, projection.shape[1])
    proj_parts = [lax.dynamic_index_in_dim(proj_blocks, p, 0, keepdims=False) for p in partners]

    tree = is_pow2(tensor_count) and tensor_count > 1 and width % 2 == 0
    half = width // 2

    def head_term(p):
        columns = lax.dynamic_slice_in_dim(out_proj, p * width, width, axis=1)
        return jnp.dot(context, columns, preferred_element_type=jnp.float32).astype(jnp.bfloat16)

    if tree:
        def head_half(d, h):
            start = (me_t ^ d) * width + h * half
            columns = lax.dynamic_slice_in_dim(out_proj, start, half, axis=1)
            return jnp.dot(context, columns, preferred_element_type=jnp.float32).astype(jnp.bfloat16)

        summed = jnp.concatenate(reduce_scatter_tree(head_half, "tensor", tensor_count), axis=1)
        summed = summed + residual_in.astype(jnp.float32)
    else:
        received = [
            lax.ppermute(head_term(partners[s]), "tensor", pairs_for(s, tensor_count))
            for s in range(1, tensor_count)
        ]
        summed = head_term(me_t).astype(jnp.float32) + residual_in.astype(jnp.float32)
        for got in received:
            summed = summed + got.astype(jnp.float32)
    generated = summed.astype(jnp.bfloat16)

    group_ids = lax.iota(jnp.int32, group_count)
    member_ids = members[:, 0]
    destination = jnp.sum(
        jnp.where(member_ids[:, None] == group_ids[None, :], host_group[None, :], 0), axis=1
    )
    dest_hot = (destination[:, None] == group_ids[None, :]).astype(jnp.int32)
    earlier = jnp.cumsum(dest_hot, axis=0) - dest_hot
    rank_in = jnp.sum(earlier * dest_hot, axis=1)
    slot_ids = lax.iota(jnp.int32, chunk_slots)
    head_row = member_head[0][None, :]

    input_grad = None
    for c in range(chunks):
        local_rank = rank_in - c * chunk_cap
        inside = (local_rank >= 0) & (local_rank < chunk_cap)
        slot_of = destination * chunk_cap + local_rank
        placing = ((slot_of[:, None] == slot_ids[None, :]) & inside[:, None]).astype(jnp.bfloat16)
        outgoing = lax.dot_general(
            placing, generated, (((0,), (0,)), ((), ())), preferred_element_type=jnp.float32
        ).astype(jnp.bfloat16)
        arrived = swap_blocks(outgoing.reshape(group_count, chunk_cap, width), "dp")
        arrived = arrived.reshape(chunk_slots, width)
        if tree:
            pre_act = None
            held = all_gather_tree([arrived[:, :half], arrived[:, half:]], "tensor", tensor_count)
            for h in range(2):
                for d in range(tensor_count):
                    rows_w = lax.dynamic_slice_in_dim(projection, (me_t ^ d) * width + h * half, half, axis=0)
                    term = jnp.dot(held[h][d], rows_w, preferred_element_type=jnp.float32)
                    pre_act = term if pre_act is None else pre_act + term
        else:
            pre_act = jnp.dot(arrived, proj_parts[0], preferred_element_type=jnp.float32)
            for s in range(1, tensor_count):
                got = lax.ppermute(arrived, "tensor", pairs_for(s, tensor_count))
                pre_act = pre_act + jnp.dot(got, proj_parts[s], preferred_element_type=jnp.float32)
        pre_grad = (-slope_times(pre_act, jnp.broadcast_to(head_row, pre_act.shape))).astype(jnp.bfloat16)
        if tree:
            def back_half(d, h):
                rows_w = lax.dynamic_slice_in_dim(projection, (me_t ^ d) * width + h * half, half, axis=0)
                return lax.dot_general(
                    pre_grad, rows_w, (((1,), (1,)), ((), ())), preferred_element_type=jnp.float32
                ).astype(jnp.bfloat16)

            critic_grad = jnp.concatenate(
                reduce_scatter_tree(back_half, "tensor", tensor_count), axis=1
            ).astype(jnp.bfloat16)
        else:
            back = [
                lax.dot_general(
                    pre_grad, part, (((1,), (1,)), ((), ())), preferred_element_type=jnp.float32
                ).astype(jnp.bfloat16)
                for part in proj_parts
            ]
            critic_grad = back[0].astype(jnp.float32)
            for s in range(1, tensor_count):
                critic_grad = critic_grad + lax.ppermute(
                    back[s], "tensor", pairs_for(s, tensor_count)
                ).astype(jnp.float32)
            critic_grad = critic_grad.astype(jnp.bfloat16)
        returned = swap_blocks(critic_grad.reshape(group_count, chunk_cap, width), "dp")
        returned = returned.reshape(chunk_slots, width)
        part = jnp.dot(placing, returned, preferred_element_type=jnp.float32)
        input_grad = part if input_grad is None else input_grad + part
    return (generated, input_grad.astype(jnp.bfloat16))


def solution(mesh):
    in_specs = (
        P("dp", "tensor"),
        P("dp", "tensor"),
        P("tensor", None),
        P("dp", None),
        P(),
        P("dp", None, "tensor"),
        P("dp", "tensor"),
    )
    out_specs = (P("dp", "tensor"), P("dp", "tensor"))
    return jax.shard_map(shards, mesh=mesh, in_specs=in_specs, out_specs=out_specs, check_vma=False)
```

```python
from functools import partial

import jax
import jax.numpy as jnp
from jax import lax
from jax.sharding import PartitionSpec as P


def slope_times(values, weights):
    _, back_fn = jax.vjp(partial(jax.nn.gelu, approximate=True), values)
    return back_fn(weights)[0]


def is_pow2(n):
    return n & (n - 1) == 0


def partner_of(me, s, n):
    return me ^ s if is_pow2(n) else (me + s) % n


def pairs_for(s, n):
    if is_pow2(n):
        return [(i, i ^ s) for i in range(n)]
    return [(i, (i + s) % n) for i in range(n)]


def sources_for(s, n):
    if is_pow2(n):
        return lambda me: me ^ s
    return lambda me: (me - s) % n


def reduce_blocks(blocks, axis):
    n = blocks.shape[0]
    me = lax.axis_index(axis)
    total = lax.dynamic_index_in_dim(blocks, me, 0, keepdims=False).astype(jnp.float32)
    for s in range(1, n):
        chunk = lax.dynamic_index_in_dim(blocks, partner_of(me, s, n), 0, keepdims=False)
        total = total + lax.ppermute(chunk, axis, pairs_for(s, n)).astype(jnp.float32)
    return total


def gather_blocks(x, axis):
    n = lax.axis_size(axis)
    me = lax.axis_index(axis)
    got = [x] + [lax.ppermute(x, axis, pairs_for(s, n)) for s in range(1, n)]
    stacked = jnp.stack(got)
    if is_pow2(n):
        order = lax.iota(jnp.int32, n) ^ me
    else:
        order = (me - lax.iota(jnp.int32, n)) % n
    return jnp.take(stacked, order, axis=0)


def swap_blocks(blocks, axis):
    n = blocks.shape[0]
    if n > 16:
        return lax.all_to_all(blocks, axis, 0, 0, tiled=True)
    me = lax.axis_index(axis)
    got = [lax.dynamic_index_in_dim(blocks, me, 0, keepdims=False)]
    for s in range(1, n):
        chunk = lax.dynamic_index_in_dim(blocks, partner_of(me, s, n), 0, keepdims=False)
        got.append(lax.ppermute(chunk, axis, pairs_for(s, n)))
    stacked = jnp.stack(got)
    if is_pow2(n):
        order = lax.iota(jnp.int32, n) ^ me
    else:
        order = (me - lax.iota(jnp.int32, n)) % n
    return jnp.take(stacked, order, axis=0)


def bit_orders(n):
    bits = [1 << i for i in range(n.bit_length() - 1)]
    return [bits, bits[::-1]]


def reduce_scatter_tree(block_fn, axis, n):
    orders = bit_orders(n)
    helds = [{d: block_fn(d, h) for d in range(n)} for h in range(len(orders))]
    for stage in range(len(orders[0])):
        payloads, keeps = [], []
        for h, order in enumerate(orders):
            bit = order[stage]
            send = sorted(d for d in helds[h] if d & bit)
            keeps.append(sorted(d for d in helds[h] if not d & bit))
            payloads.append(jnp.concatenate([helds[h][d].astype(jnp.bfloat16) for d in send], axis=0))
        payloads = lax.optimization_barrier(payloads)
        for h, order in enumerate(orders):
            bit = order[stage]
            got = lax.ppermute(payloads[h], axis, [(i, i ^ bit) for i in range(n)])
            rows = helds[h][keeps[h][0]].shape[0]
            helds[h] = {
                d: helds[h][d].astype(jnp.float32) + got[i * rows:(i + 1) * rows].astype(jnp.float32)
                for i, d in enumerate(keeps[h])
            }
    return [held[0] for held in helds]


def all_gather_tree(halves, axis, n):
    orders = bit_orders(n)
    helds = [{0: halves[h]} for h in range(len(orders))]
    for stage in range(len(orders[0])):
        haves = [sorted(held) for held in helds]
        payloads = [jnp.concatenate([helds[h][d] for d in haves[h]], axis=0) for h in range(len(orders))]
        payloads = lax.optimization_barrier(payloads)
        for h, order in enumerate(orders):
            bit = order[stage]
            got = lax.ppermute(payloads[h], axis, [(i, i ^ bit) for i in range(n)])
            rows = halves[h].shape[0]
            for i, d in enumerate(haves[h]):
                helds[h][d ^ bit] = got[i * rows:(i + 1) * rows]
    return helds


def reduce_scatter_free(block_fn, axis, n):
    outs = []
    for h, order in enumerate(bit_orders(n)):
        held = {d: block_fn(d, h) for d in range(n)}
        for bit in order:
            send = sorted(d for d in held if d & bit)
            keep = sorted(d for d in held if not d & bit)
            payload = jnp.concatenate([held[d].astype(jnp.bfloat16) for d in send], axis=0)
            got = lax.ppermute(payload, axis, [(i, i ^ bit) for i in range(n)])
            rows = held[keep[0]].shape[0]
            held = {
                d: held[d].astype(jnp.float32) + got[i * rows:(i + 1) * rows].astype(jnp.float32)
                for i, d in enumerate(keep)
            }
        outs.append(held[0])
    return outs


def all_gather_free(halves, axis, n):
    outs = []
    for h, order in enumerate(bit_orders(n)):
        held = {0: halves[h]}
        for bit in order:
            have = sorted(held)
            payload = jnp.concatenate([held[d] for d in have], axis=0)
            got = lax.ppermute(payload, axis, [(i, i ^ bit) for i in range(n)])
            rows = halves[h].shape[0]
            for i, d in enumerate(have):
                held[d ^ bit] = got[i * rows:(i + 1) * rows]
        outs.append(held)
    return outs


SLOT_CHUNKS = 1


def shards(context, residual_in, out_proj, members, host_group, member_proj, member_head):
    tok_rows, width = context.shape
    group_count = lax.axis_size("dp")
    tensor_count = lax.axis_size("tensor")
    capacity = max(2, (5 * tok_rows + 4 * group_count - 1) // (4 * group_count))
    chunks = SLOT_CHUNKS if capacity % SLOT_CHUNKS == 0 else 1
    chunk_cap = capacity // chunks
    chunk_slots = group_count * chunk_cap
    me_t = lax.axis_index("tensor")
    partners = [partner_of(me_t, s, tensor_count) for s in range(tensor_count)]
    projection = member_proj[0]
    proj_blocks = projection.reshape(tensor_count, width, projection.shape[1])
    proj_parts = [lax.dynamic_index_in_dim(proj_blocks, p, 0, keepdims=False) for p in partners]

    tree = is_pow2(tensor_count) and tensor_count > 1 and width % 2 == 0
    half = width // 2

    def head_term(p):
        columns = lax.dynamic_slice_in_dim(out_proj, p * width, width, axis=1)
        return jnp.dot(context, columns, preferred_element_type=jnp.float32).astype(jnp.bfloat16)

    if tree:
        head_cols = lax.dot_general(
            out_proj, context, (((0,), (1,)), ((), ())), preferred_element_type=jnp.float32
        ).astype(jnp.bfloat16)

        def head_half(d, h):
            return lax.dynamic_slice_in_dim(head_cols, (me_t ^ d) * width + h * half, half, axis=0)

        summed = jnp.concatenate(reduce_scatter_tree(head_half, "tensor", tensor_count), axis=0).T
        summed = summed + residual_in.astype(jnp.float32)
    else:
        received = [
            lax.ppermute(head_term(partners[s]), "tensor", pairs_for(s, tensor_count))
            for s in range(1, tensor_count)
        ]
        summed = head_term(me_t).astype(jnp.float32) + residual_in.astype(jnp.float32)
        for got in received:
            summed = summed + got.astype(jnp.float32)
    generated = summed.astype(jnp.bfloat16)

    group_ids = lax.iota(jnp.int32, group_count)
    member_ids = members[:, 0]
    destination = jnp.sum(
        jnp.where(member_ids[:, None] == group_ids[None, :], host_group[None, :], 0), axis=1
    )
    dest_hot = (destination[:, None] == group_ids[None, :]).astype(jnp.int32)
    earlier = jnp.cumsum(dest_hot, axis=0) - dest_hot
    rank_in = jnp.sum(earlier * dest_hot, axis=1)
    slot_ids = lax.iota(jnp.int32, chunk_slots)
    head_row = member_head[0][None, :]

    input_grad = None
    for c in range(chunks):
        local_rank = rank_in - c * chunk_cap
        inside = (local_rank >= 0) & (local_rank < chunk_cap)
        slot_of = destination * chunk_cap + local_rank
        placing = ((slot_of[:, None] == slot_ids[None, :]) & inside[:, None]).astype(jnp.bfloat16)
        outgoing = lax.dot_general(
            placing, generated, (((0,), (0,)), ((), ())), preferred_element_type=jnp.float32
        ).astype(jnp.bfloat16)
        arrived = swap_blocks(outgoing.reshape(group_count, chunk_cap, width), "dp")
        arrived = arrived.reshape(chunk_slots, width)
        if tree:
            pre_act = None
            held = all_gather_free([arrived[:, :half], arrived[:, half:]], "tensor", tensor_count)
            for h in range(2):
                for d in range(tensor_count):
                    rows_w = lax.dynamic_slice_in_dim(projection, (me_t ^ d) * width + h * half, half, axis=0)
                    term = jnp.dot(held[h][d], rows_w, preferred_element_type=jnp.float32)
                    pre_act = term if pre_act is None else pre_act + term
        else:
            pre_act = jnp.dot(arrived, proj_parts[0], preferred_element_type=jnp.float32)
            for s in range(1, tensor_count):
                got = lax.ppermute(arrived, "tensor", pairs_for(s, tensor_count))
                pre_act = pre_act + jnp.dot(got, proj_parts[s], preferred_element_type=jnp.float32)
        pre_grad = (-slope_times(pre_act, jnp.broadcast_to(head_row, pre_act.shape))).astype(jnp.bfloat16)
        if tree:
            def back_half(d, h):
                rows_w = lax.dynamic_slice_in_dim(projection, (me_t ^ d) * width + h * half, half, axis=0)
                return lax.dot_general(
                    pre_grad, rows_w, (((1,), (1,)), ((), ())), preferred_element_type=jnp.float32
                ).astype(jnp.bfloat16)

            critic_grad = jnp.concatenate(
                reduce_scatter_free(back_half, "tensor", tensor_count), axis=1
            ).astype(jnp.bfloat16)
        else:
            back = [
                lax.dot_general(
                    pre_grad, part, (((1,), (1,)), ((), ())), preferred_element_type=jnp.float32
                ).astype(jnp.bfloat16)
                for part in proj_parts
            ]
            critic_grad = back[0].astype(jnp.float32)
            for s in range(1, tensor_count):
                critic_grad = critic_grad + lax.ppermute(
                    back[s], "tensor", pairs_for(s, tensor_count)
                ).astype(jnp.float32)
            critic_grad = critic_grad.astype(jnp.bfloat16)
        returned = swap_blocks(critic_grad.reshape(group_count, chunk_cap, width), "dp")
        returned = returned.reshape(chunk_slots, width)
        part = jnp.dot(placing, returned, preferred_element_type=jnp.float32)
        input_grad = part if input_grad is None else input_grad + part
    return (generated, input_grad.astype(jnp.bfloat16))


def solution(mesh):
    in_specs = (
        P("dp", "tensor"),
        P("dp", "tensor"),
        P("tensor", None),
        P("dp", None),
        P(),
        P("dp", None, "tensor"),
        P("dp", "tensor"),
    )
    out_specs = (P("dp", "tensor"), P("dp", "tensor"))
    return jax.shard_map(shards, mesh=mesh, in_specs=in_specs, out_specs=out_specs, check_vma=False)
```

```python
from functools import partial

import jax
import jax.numpy as jnp
from jax import lax
from jax.sharding import PartitionSpec as P


def slope_times(values, weights):
    _, back_fn = jax.vjp(partial(jax.nn.gelu, approximate=True), values)
    return back_fn(weights)[0]


def is_pow2(n):
    return n & (n - 1) == 0


def partner_of(me, s, n):
    return me ^ s if is_pow2(n) else (me + s) % n


def pairs_for(s, n):
    if is_pow2(n):
        return [(i, i ^ s) for i in range(n)]
    return [(i, (i + s) % n) for i in range(n)]


def sources_for(s, n):
    if is_pow2(n):
        return lambda me: me ^ s
    return lambda me: (me - s) % n


def reduce_blocks(blocks, axis):
    n = blocks.shape[0]
    me = lax.axis_index(axis)
    total = lax.dynamic_index_in_dim(blocks, me, 0, keepdims=False).astype(jnp.float32)
    for s in range(1, n):
        chunk = lax.dynamic_index_in_dim(blocks, partner_of(me, s, n), 0, keepdims=False)
        total = total + lax.ppermute(chunk, axis, pairs_for(s, n)).astype(jnp.float32)
    return total


def gather_blocks(x, axis):
    n = lax.axis_size(axis)
    me = lax.axis_index(axis)
    got = [x] + [lax.ppermute(x, axis, pairs_for(s, n)) for s in range(1, n)]
    stacked = jnp.stack(got)
    if is_pow2(n):
        order = lax.iota(jnp.int32, n) ^ me
    else:
        order = (me - lax.iota(jnp.int32, n)) % n
    return jnp.take(stacked, order, axis=0)


def swap_blocks(blocks, axis):
    n = blocks.shape[0]
    if n > 16:
        return lax.all_to_all(blocks, axis, 0, 0, tiled=True)
    me = lax.axis_index(axis)
    got = [lax.dynamic_index_in_dim(blocks, me, 0, keepdims=False)]
    for s in range(1, n):
        chunk = lax.dynamic_index_in_dim(blocks, partner_of(me, s, n), 0, keepdims=False)
        got.append(lax.ppermute(chunk, axis, pairs_for(s, n)))
    stacked = jnp.stack(got)
    if is_pow2(n):
        order = lax.iota(jnp.int32, n) ^ me
    else:
        order = (me - lax.iota(jnp.int32, n)) % n
    return jnp.take(stacked, order, axis=0)


def bit_orders(n):
    bits = [1 << i for i in range(n.bit_length() - 1)]
    return [bits, bits[::-1]]


def reduce_scatter_tree(block_fn, axis, n):
    orders = bit_orders(n)
    helds = [{d: block_fn(d, h) for d in range(n)} for h in range(len(orders))]
    for stage in range(len(orders[0])):
        payloads, keeps = [], []
        for h, order in enumerate(orders):
            bit = order[stage]
            send = sorted(d for d in helds[h] if d & bit)
            keeps.append(sorted(d for d in helds[h] if not d & bit))
            payloads.append(jnp.concatenate([helds[h][d].astype(jnp.bfloat16) for d in send], axis=0))
        payloads = lax.optimization_barrier(payloads)
        for h, order in enumerate(orders):
            bit = order[stage]
            got = lax.ppermute(payloads[h], axis, [(i, i ^ bit) for i in range(n)])
            rows = helds[h][keeps[h][0]].shape[0]
            helds[h] = {
                d: helds[h][d].astype(jnp.float32) + got[i * rows:(i + 1) * rows].astype(jnp.float32)
                for i, d in enumerate(keeps[h])
            }
    return [held[0] for held in helds]


def all_gather_tree(halves, axis, n):
    orders = bit_orders(n)
    helds = [{0: halves[h]} for h in range(len(orders))]
    for stage in range(len(orders[0])):
        haves = [sorted(held) for held in helds]
        payloads = [jnp.concatenate([helds[h][d] for d in haves[h]], axis=0) for h in range(len(orders))]
        payloads = lax.optimization_barrier(payloads)
        for h, order in enumerate(orders):
            bit = order[stage]
            got = lax.ppermute(payloads[h], axis, [(i, i ^ bit) for i in range(n)])
            rows = halves[h].shape[0]
            for i, d in enumerate(haves[h]):
                helds[h][d ^ bit] = got[i * rows:(i + 1) * rows]
    return helds


def reduce_scatter_free(block_fn, axis, n):
    outs = []
    for h, order in enumerate(bit_orders(n)):
        held = {d: block_fn(d, h) for d in range(n)}
        for bit in order:
            send = sorted(d for d in held if d & bit)
            keep = sorted(d for d in held if not d & bit)
            payload = jnp.concatenate([held[d].astype(jnp.bfloat16) for d in send], axis=0)
            got = lax.ppermute(payload, axis, [(i, i ^ bit) for i in range(n)])
            rows = held[keep[0]].shape[0]
            held = {
                d: held[d].astype(jnp.float32) + got[i * rows:(i + 1) * rows].astype(jnp.float32)
                for i, d in enumerate(keep)
            }
        outs.append(held[0])
    return outs


def all_gather_free(halves, axis, n):
    outs = []
    for h, order in enumerate(bit_orders(n)):
        held = {0: halves[h]}
        for bit in order:
            have = sorted(held)
            payload = jnp.concatenate([held[d] for d in have], axis=0)
            got = lax.ppermute(payload, axis, [(i, i ^ bit) for i in range(n)])
            rows = halves[h].shape[0]
            for i, d in enumerate(have):
                held[d ^ bit] = got[i * rows:(i + 1) * rows]
        outs.append(held)
    return outs


def dispatch_rows(blocks, axis):
    n = blocks.shape[0]
    if n > 16 or not is_pow2(n):
        arrived = lax.all_to_all(blocks, axis, 0, 0, tiled=True)
        return [arrived[p] for p in range(n)]
    me = lax.axis_index(axis)
    got = [lax.dynamic_index_in_dim(blocks, me, 0, keepdims=False)]
    for s in range(1, n):
        chunk = lax.dynamic_index_in_dim(blocks, me ^ s, 0, keepdims=False)
        got.append(lax.ppermute(chunk, axis, [(i, i ^ s) for i in range(n)]))
    return got


def collect_rows(parts, axis):
    n = len(parts)
    if n > 16 or not is_pow2(n):
        return lax.all_to_all(jnp.stack(parts), axis, 0, 0, tiled=True)
    me = lax.axis_index(axis)
    got = [parts[0]] + [
        lax.ppermute(parts[s], axis, [(i, i ^ s) for i in range(n)]) for s in range(1, n)
    ]
    return jnp.take(jnp.stack(got), lax.iota(jnp.int32, n) ^ me, axis=0)


SLOT_CHUNKS = 1


def shards(context, residual_in, out_proj, members, host_group, member_proj, member_head):
    tok_rows, width = context.shape
    group_count = lax.axis_size("dp")
    tensor_count = lax.axis_size("tensor")
    capacity = max(2, (5 * tok_rows + 4 * group_count - 1) // (4 * group_count))
    chunks = SLOT_CHUNKS if capacity % SLOT_CHUNKS == 0 else 1
    chunk_cap = capacity // chunks
    chunk_slots = group_count * chunk_cap
    me_t = lax.axis_index("tensor")
    partners = [partner_of(me_t, s, tensor_count) for s in range(tensor_count)]
    projection = member_proj[0]
    proj_blocks = projection.reshape(tensor_count, width, projection.shape[1])
    proj_parts = [lax.dynamic_index_in_dim(proj_blocks, p, 0, keepdims=False) for p in partners]

    tree = is_pow2(tensor_count) and tensor_count > 1 and width % 2 == 0
    half = width // 2

    def head_term(p):
        columns = lax.dynamic_slice_in_dim(out_proj, p * width, width, axis=1)
        return jnp.dot(context, columns, preferred_element_type=jnp.float32).astype(jnp.bfloat16)

    if tree:
        head_cols = lax.dot_general(
            out_proj, context, (((0,), (1,)), ((), ())), preferred_element_type=jnp.float32
        ).astype(jnp.bfloat16)

        def head_half(d, h):
            return lax.dynamic_slice_in_dim(head_cols, (me_t ^ d) * width + h * half, half, axis=0)

        summed = jnp.concatenate(reduce_scatter_tree(head_half, "tensor", tensor_count), axis=0).T
        summed = summed + residual_in.astype(jnp.float32)
    else:
        received = [
            lax.ppermute(head_term(partners[s]), "tensor", pairs_for(s, tensor_count))
            for s in range(1, tensor_count)
        ]
        summed = head_term(me_t).astype(jnp.float32) + residual_in.astype(jnp.float32)
        for got in received:
            summed = summed + got.astype(jnp.float32)
    generated = summed.astype(jnp.bfloat16)

    group_ids = lax.iota(jnp.int32, group_count)
    member_ids = members[:, 0]
    destination = jnp.sum(
        jnp.where(member_ids[:, None] == group_ids[None, :], host_group[None, :], 0), axis=1
    )
    dest_hot = (destination[:, None] == group_ids[None, :]).astype(jnp.int32)
    earlier = jnp.cumsum(dest_hot, axis=0) - dest_hot
    rank_in = jnp.sum(earlier * dest_hot, axis=1)
    slot_ids = lax.iota(jnp.int32, chunk_slots)
    head_row = member_head[0][None, :]

    if tree:
        rank_ok = rank_in < capacity
        slot_of = destination * capacity + rank_in
        placing = ((slot_of[:, None] == lax.iota(jnp.int32, group_count * capacity)[None, :])
                   & rank_ok[:, None]).astype(jnp.bfloat16)
        outgoing = lax.dot_general(
            placing, generated, (((0,), (0,)), ((), ())), preferred_element_type=jnp.float32
        ).astype(jnp.bfloat16)
        arrived = dispatch_rows(outgoing.reshape(group_count, capacity, width), "dp")
        wave = max(1, group_count // 2)
        waves = [arrived[:wave], arrived[wave:]] if group_count > 1 else [arrived]
        grads = []
        for blocks in waves:
            rows_in = jnp.concatenate(blocks, axis=0)
            held = all_gather_free([rows_in[:, :half], rows_in[:, half:]], "tensor", tensor_count)
            pre_act = None
            for h in range(2):
                for d in range(tensor_count):
                    rows_w = lax.dynamic_slice_in_dim(projection, (me_t ^ d) * width + h * half, half, axis=0)
                    term = jnp.dot(held[h][d], rows_w, preferred_element_type=jnp.float32)
                    pre_act = term if pre_act is None else pre_act + term
            pre_grad = (-slope_times(pre_act, jnp.broadcast_to(head_row, pre_act.shape))).astype(jnp.bfloat16)

            def back_half(d, h, pre_grad=pre_grad):
                rows_w = lax.dynamic_slice_in_dim(projection, (me_t ^ d) * width + h * half, half, axis=0)
                return lax.dot_general(
                    pre_grad, rows_w, (((1,), (1,)), ((), ())), preferred_element_type=jnp.float32
                ).astype(jnp.bfloat16)

            grad = jnp.concatenate(
                reduce_scatter_free(back_half, "tensor", tensor_count), axis=1
            ).astype(jnp.bfloat16)
            grads.extend(jnp.split(grad, len(blocks), axis=0))
        returned = collect_rows(grads, "dp").reshape(group_count * capacity, width)
        input_grad = jnp.dot(placing, returned, preferred_element_type=jnp.float32)
        return (generated, input_grad.astype(jnp.bfloat16))

    input_grad = None
    for c in range(chunks):
        local_rank = rank_in - c * chunk_cap
        inside = (local_rank >= 0) & (local_rank < chunk_cap)
        slot_of = destination * chunk_cap + local_rank
        placing = ((slot_of[:, None] == slot_ids[None, :]) & inside[:, None]).astype(jnp.bfloat16)
        outgoing = lax.dot_general(
            placing, generated, (((0,), (0,)), ((), ())), preferred_element_type=jnp.float32
        ).astype(jnp.bfloat16)
        arrived = swap_blocks(outgoing.reshape(group_count, chunk_cap, width), "dp")
        arrived = arrived.reshape(chunk_slots, width)
        if tree:
            pre_act = None
            held = all_gather_free([arrived[:, :half], arrived[:, half:]], "tensor", tensor_count)
            for h in range(2):
                for d in range(tensor_count):
                    rows_w = lax.dynamic_slice_in_dim(projection, (me_t ^ d) * width + h * half, half, axis=0)
                    term = jnp.dot(held[h][d], rows_w, preferred_element_type=jnp.float32)
                    pre_act = term if pre_act is None else pre_act + term
        else:
            pre_act = jnp.dot(arrived, proj_parts[0], preferred_element_type=jnp.float32)
            for s in range(1, tensor_count):
                got = lax.ppermute(arrived, "tensor", pairs_for(s, tensor_count))
                pre_act = pre_act + jnp.dot(got, proj_parts[s], preferred_element_type=jnp.float32)
        pre_grad = (-slope_times(pre_act, jnp.broadcast_to(head_row, pre_act.shape))).astype(jnp.bfloat16)
        if tree:
            def back_half(d, h):
                rows_w = lax.dynamic_slice_in_dim(projection, (me_t ^ d) * width + h * half, half, axis=0)
                return lax.dot_general(
                    pre_grad, rows_w, (((1,), (1,)), ((), ())), preferred_element_type=jnp.float32
                ).astype(jnp.bfloat16)

            critic_grad = jnp.concatenate(
                reduce_scatter_free(back_half, "tensor", tensor_count), axis=1
            ).astype(jnp.bfloat16)
        else:
            back = [
                lax.dot_general(
                    pre_grad, part, (((1,), (1,)), ((), ())), preferred_element_type=jnp.float32
                ).astype(jnp.bfloat16)
                for part in proj_parts
            ]
            critic_grad = back[0].astype(jnp.float32)
            for s in range(1, tensor_count):
                critic_grad = critic_grad + lax.ppermute(
                    back[s], "tensor", pairs_for(s, tensor_count)
                ).astype(jnp.float32)
            critic_grad = critic_grad.astype(jnp.bfloat16)
        returned = swap_blocks(critic_grad.reshape(group_count, chunk_cap, width), "dp")
        returned = returned.reshape(chunk_slots, width)
        part = jnp.dot(placing, returned, preferred_element_type=jnp.float32)
        input_grad = part if input_grad is None else input_grad + part
    return (generated, input_grad.astype(jnp.bfloat16))


def solution(mesh):
    in_specs = (
        P("dp", "tensor"),
        P("dp", "tensor"),
        P("tensor", None),
        P("dp", None),
        P(),
        P("dp", None, "tensor"),
        P("dp", "tensor"),
    )
    out_specs = (P("dp", "tensor"), P("dp", "tensor"))
    return jax.shard_map(shards, mesh=mesh, in_specs=in_specs, out_specs=out_specs, check_vma=False)
```

```python
from functools import partial

import jax
import jax.numpy as jnp
from jax import lax
from jax.sharding import PartitionSpec as P


def slope_times(values, weights):
    _, back_fn = jax.vjp(partial(jax.nn.gelu, approximate=True), values)
    return back_fn(weights)[0]


def is_pow2(n):
    return n & (n - 1) == 0


def partner_of(me, s, n):
    return me ^ s if is_pow2(n) else (me + s) % n


def pairs_for(s, n):
    if is_pow2(n):
        return [(i, i ^ s) for i in range(n)]
    return [(i, (i + s) % n) for i in range(n)]


def sources_for(s, n):
    if is_pow2(n):
        return lambda me: me ^ s
    return lambda me: (me - s) % n


def reduce_blocks(blocks, axis):
    n = blocks.shape[0]
    me = lax.axis_index(axis)
    total = lax.dynamic_index_in_dim(blocks, me, 0, keepdims=False).astype(jnp.float32)
    for s in range(1, n):
        chunk = lax.dynamic_index_in_dim(blocks, partner_of(me, s, n), 0, keepdims=False)
        total = total + lax.ppermute(chunk, axis, pairs_for(s, n)).astype(jnp.float32)
    return total


def gather_blocks(x, axis):
    n = lax.axis_size(axis)
    me = lax.axis_index(axis)
    got = [x] + [lax.ppermute(x, axis, pairs_for(s, n)) for s in range(1, n)]
    stacked = jnp.stack(got)
    if is_pow2(n):
        order = lax.iota(jnp.int32, n) ^ me
    else:
        order = (me - lax.iota(jnp.int32, n)) % n
    return jnp.take(stacked, order, axis=0)


def swap_blocks(blocks, axis):
    n = blocks.shape[0]
    if n > 16:
        return lax.all_to_all(blocks, axis, 0, 0, tiled=True)
    me = lax.axis_index(axis)
    got = [lax.dynamic_index_in_dim(blocks, me, 0, keepdims=False)]
    for s in range(1, n):
        chunk = lax.dynamic_index_in_dim(blocks, partner_of(me, s, n), 0, keepdims=False)
        got.append(lax.ppermute(chunk, axis, pairs_for(s, n)))
    stacked = jnp.stack(got)
    if is_pow2(n):
        order = lax.iota(jnp.int32, n) ^ me
    else:
        order = (me - lax.iota(jnp.int32, n)) % n
    return jnp.take(stacked, order, axis=0)


def bit_orders(n):
    bits = [1 << i for i in range(n.bit_length() - 1)]
    return [bits, bits[::-1]]


def reduce_scatter_tree(block_fn, axis, n):
    orders = bit_orders(n)
    helds = [{d: block_fn(d, h) for d in range(n)} for h in range(len(orders))]
    for stage in range(len(orders[0])):
        payloads, keeps = [], []
        for h, order in enumerate(orders):
            bit = order[stage]
            send = sorted(d for d in helds[h] if d & bit)
            keeps.append(sorted(d for d in helds[h] if not d & bit))
            payloads.append(jnp.concatenate([helds[h][d].astype(jnp.bfloat16) for d in send], axis=0))
        payloads = lax.optimization_barrier(payloads)
        for h, order in enumerate(orders):
            bit = order[stage]
            got = lax.ppermute(payloads[h], axis, [(i, i ^ bit) for i in range(n)])
            rows = helds[h][keeps[h][0]].shape[0]
            helds[h] = {
                d: helds[h][d].astype(jnp.float32) + got[i * rows:(i + 1) * rows].astype(jnp.float32)
                for i, d in enumerate(keeps[h])
            }
    return [held[0] for held in helds]


def all_gather_tree(halves, axis, n):
    orders = bit_orders(n)
    helds = [{0: halves[h]} for h in range(len(orders))]
    for stage in range(len(orders[0])):
        haves = [sorted(held) for held in helds]
        payloads = [jnp.concatenate([helds[h][d] for d in haves[h]], axis=0) for h in range(len(orders))]
        payloads = lax.optimization_barrier(payloads)
        for h, order in enumerate(orders):
            bit = order[stage]
            got = lax.ppermute(payloads[h], axis, [(i, i ^ bit) for i in range(n)])
            rows = halves[h].shape[0]
            for i, d in enumerate(haves[h]):
                helds[h][d ^ bit] = got[i * rows:(i + 1) * rows]
    return helds


def reduce_scatter_free(block_fn, axis, n):
    outs = []
    for h, order in enumerate(bit_orders(n)):
        held = {d: block_fn(d, h) for d in range(n)}
        for bit in order:
            send = sorted(d for d in held if d & bit)
            keep = sorted(d for d in held if not d & bit)
            payload = jnp.concatenate([held[d].astype(jnp.bfloat16) for d in send], axis=0)
            got = lax.ppermute(payload, axis, [(i, i ^ bit) for i in range(n)])
            rows = held[keep[0]].shape[0]
            held = {
                d: held[d].astype(jnp.float32) + got[i * rows:(i + 1) * rows].astype(jnp.float32)
                for i, d in enumerate(keep)
            }
        outs.append(held[0])
    return outs


def all_gather_free(halves, axis, n):
    outs = []
    for h, order in enumerate(bit_orders(n)):
        held = {0: halves[h]}
        for bit in order:
            have = sorted(held)
            payload = jnp.concatenate([held[d] for d in have], axis=0)
            got = lax.ppermute(payload, axis, [(i, i ^ bit) for i in range(n)])
            rows = halves[h].shape[0]
            for i, d in enumerate(have):
                held[d ^ bit] = got[i * rows:(i + 1) * rows]
        outs.append(held)
    return outs


def dispatch_rows(blocks, axis):
    n = blocks.shape[0]
    if n > 16 or not is_pow2(n):
        arrived = lax.all_to_all(blocks, axis, 0, 0, tiled=True)
        return [arrived[p] for p in range(n)]
    me = lax.axis_index(axis)
    got = [lax.dynamic_index_in_dim(blocks, me, 0, keepdims=False)]
    for s in range(1, n):
        chunk = lax.dynamic_index_in_dim(blocks, me ^ s, 0, keepdims=False)
        got.append(lax.ppermute(chunk, axis, [(i, i ^ s) for i in range(n)]))
    return got


def collect_rows(parts, axis):
    n = len(parts)
    if n > 16 or not is_pow2(n):
        return lax.all_to_all(jnp.stack(parts), axis, 0, 0, tiled=True)
    me = lax.axis_index(axis)
    got = [parts[0]] + [
        lax.ppermute(parts[s], axis, [(i, i ^ s) for i in range(n)]) for s in range(1, n)
    ]
    return jnp.take(jnp.stack(got), lax.iota(jnp.int32, n) ^ me, axis=0)


SLOT_CHUNKS = 1


def shards(context, residual_in, out_proj, members, host_group, member_proj, member_head):
    tok_rows, width = context.shape
    group_count = lax.axis_size("dp")
    tensor_count = lax.axis_size("tensor")
    capacity = max(2, (5 * tok_rows + 4 * group_count - 1) // (4 * group_count))
    chunks = SLOT_CHUNKS if capacity % SLOT_CHUNKS == 0 else 1
    chunk_cap = capacity // chunks
    chunk_slots = group_count * chunk_cap
    me_t = lax.axis_index("tensor")
    partners = [partner_of(me_t, s, tensor_count) for s in range(tensor_count)]
    projection = member_proj[0]
    proj_blocks = projection.reshape(tensor_count, width, projection.shape[1])
    proj_parts = [lax.dynamic_index_in_dim(proj_blocks, p, 0, keepdims=False) for p in partners]

    tree = is_pow2(tensor_count) and tensor_count > 1 and width % 2 == 0
    half = width // 2

    def head_term(p):
        columns = lax.dynamic_slice_in_dim(out_proj, p * width, width, axis=1)
        return jnp.dot(context, columns, preferred_element_type=jnp.float32).astype(jnp.bfloat16)

    if tree:
        head_rows = jnp.dot(context, out_proj, preferred_element_type=jnp.float32).astype(jnp.bfloat16)
        row_half = tok_rows // 2

        def head_half(d, h):
            rows = head_rows[h * row_half:(h + 1) * row_half]
            return lax.dynamic_slice_in_dim(rows, (me_t ^ d) * width, width, axis=1)

        summed = jnp.concatenate(reduce_scatter_tree(head_half, "tensor", tensor_count), axis=0)
        summed = summed + residual_in.astype(jnp.float32)
    else:
        received = [
            lax.ppermute(head_term(partners[s]), "tensor", pairs_for(s, tensor_count))
            for s in range(1, tensor_count)
        ]
        summed = head_term(me_t).astype(jnp.float32) + residual_in.astype(jnp.float32)
        for got in received:
            summed = summed + got.astype(jnp.float32)
    generated = summed.astype(jnp.bfloat16)

    group_ids = lax.iota(jnp.int32, group_count)
    member_ids = members[:, 0]
    destination = jnp.sum(
        jnp.where(member_ids[:, None] == group_ids[None, :], host_group[None, :], 0), axis=1
    )
    dest_hot = (destination[:, None] == group_ids[None, :]).astype(jnp.int32)
    earlier = jnp.cumsum(dest_hot, axis=0) - dest_hot
    rank_in = jnp.sum(earlier * dest_hot, axis=1)
    slot_ids = lax.iota(jnp.int32, chunk_slots)
    head_row = member_head[0][None, :]

    if tree:
        rank_ok = rank_in < capacity
        slot_of = destination * capacity + rank_in
        placing = ((slot_of[:, None] == lax.iota(jnp.int32, group_count * capacity)[None, :])
                   & rank_ok[:, None]).astype(jnp.bfloat16)
        outgoing = lax.dot_general(
            placing, generated, (((0,), (0,)), ((), ())), preferred_element_type=jnp.float32
        ).astype(jnp.bfloat16)
        arrived = dispatch_rows(outgoing.reshape(group_count, capacity, width), "dp")
        wave = max(1, group_count // 2)
        waves = [arrived[:wave], arrived[wave:]] if group_count > 1 else [arrived]
        grads = []
        for blocks in waves:
            rows_in = jnp.concatenate(blocks, axis=0)
            held = all_gather_free([rows_in[:, :half], rows_in[:, half:]], "tensor", tensor_count)
            pre_act = None
            for h in range(2):
                for d in range(tensor_count):
                    rows_w = lax.dynamic_slice_in_dim(projection, (me_t ^ d) * width + h * half, half, axis=0)
                    term = jnp.dot(held[h][d], rows_w, preferred_element_type=jnp.float32)
                    pre_act = term if pre_act is None else pre_act + term
            pre_grad = (-slope_times(pre_act, jnp.broadcast_to(head_row, pre_act.shape))).astype(jnp.bfloat16)

            def back_half(d, h, pre_grad=pre_grad):
                rows_w = lax.dynamic_slice_in_dim(projection, (me_t ^ d) * width + h * half, half, axis=0)
                return lax.dot_general(
                    pre_grad, rows_w, (((1,), (1,)), ((), ())), preferred_element_type=jnp.float32
                ).astype(jnp.bfloat16)

            grad = jnp.concatenate(
                reduce_scatter_free(back_half, "tensor", tensor_count), axis=1
            ).astype(jnp.bfloat16)
            grads.extend(jnp.split(grad, len(blocks), axis=0))
        returned = collect_rows(grads, "dp").reshape(group_count * capacity, width)
        input_grad = jnp.dot(placing, returned, preferred_element_type=jnp.float32)
        return (generated, input_grad.astype(jnp.bfloat16))

    input_grad = None
    for c in range(chunks):
        local_rank = rank_in - c * chunk_cap
        inside = (local_rank >= 0) & (local_rank < chunk_cap)
        slot_of = destination * chunk_cap + local_rank
        placing = ((slot_of[:, None] == slot_ids[None, :]) & inside[:, None]).astype(jnp.bfloat16)
        outgoing = lax.dot_general(
            placing, generated, (((0,), (0,)), ((), ())), preferred_element_type=jnp.float32
        ).astype(jnp.bfloat16)
        arrived = swap_blocks(outgoing.reshape(group_count, chunk_cap, width), "dp")
        arrived = arrived.reshape(chunk_slots, width)
        if tree:
            pre_act = None
            held = all_gather_free([arrived[:, :half], arrived[:, half:]], "tensor", tensor_count)
            for h in range(2):
                for d in range(tensor_count):
                    rows_w = lax.dynamic_slice_in_dim(projection, (me_t ^ d) * width + h * half, half, axis=0)
                    term = jnp.dot(held[h][d], rows_w, preferred_element_type=jnp.float32)
                    pre_act = term if pre_act is None else pre_act + term
        else:
            pre_act = jnp.dot(arrived, proj_parts[0], preferred_element_type=jnp.float32)
            for s in range(1, tensor_count):
                got = lax.ppermute(arrived, "tensor", pairs_for(s, tensor_count))
                pre_act = pre_act + jnp.dot(got, proj_parts[s], preferred_element_type=jnp.float32)
        pre_grad = (-slope_times(pre_act, jnp.broadcast_to(head_row, pre_act.shape))).astype(jnp.bfloat16)
        if tree:
            def back_half(d, h):
                rows_w = lax.dynamic_slice_in_dim(projection, (me_t ^ d) * width + h * half, half, axis=0)
                return lax.dot_general(
                    pre_grad, rows_w, (((1,), (1,)), ((), ())), preferred_element_type=jnp.float32
                ).astype(jnp.bfloat16)

            critic_grad = jnp.concatenate(
                reduce_scatter_free(back_half, "tensor", tensor_count), axis=1
            ).astype(jnp.bfloat16)
        else:
            back = [
                lax.dot_general(
                    pre_grad, part, (((1,), (1,)), ((), ())), preferred_element_type=jnp.float32
                ).astype(jnp.bfloat16)
                for part in proj_parts
            ]
            critic_grad = back[0].astype(jnp.float32)
            for s in range(1, tensor_count):
                critic_grad = critic_grad + lax.ppermute(
                    back[s], "tensor", pairs_for(s, tensor_count)
                ).astype(jnp.float32)
            critic_grad = critic_grad.astype(jnp.bfloat16)
        returned = swap_blocks(critic_grad.reshape(group_count, chunk_cap, width), "dp")
        returned = returned.reshape(chunk_slots, width)
        part = jnp.dot(placing, returned, preferred_element_type=jnp.float32)
        input_grad = part if input_grad is None else input_grad + part
    return (generated, input_grad.astype(jnp.bfloat16))


def solution(mesh):
    in_specs = (
        P("dp", "tensor"),
        P("dp", "tensor"),
        P("tensor", None),
        P("dp", None),
        P(),
        P("dp", None, "tensor"),
        P("dp", "tensor"),
    )
    out_specs = (P("dp", "tensor"), P("dp", "tensor"))
    return jax.shard_map(shards, mesh=mesh, in_specs=in_specs, out_specs=out_specs, check_vma=False)
```

```python
from functools import partial

import jax
import jax.numpy as jnp
from jax import lax
from jax.sharding import PartitionSpec as P


def slope_times(values, weights):
    _, back_fn = jax.vjp(partial(jax.nn.gelu, approximate=True), values)
    return back_fn(weights)[0]


def is_pow2(n):
    return n & (n - 1) == 0


def partner_of(me, s, n):
    return me ^ s if is_pow2(n) else (me + s) % n


def pairs_for(s, n):
    if is_pow2(n):
        return [(i, i ^ s) for i in range(n)]
    return [(i, (i + s) % n) for i in range(n)]


def sources_for(s, n):
    if is_pow2(n):
        return lambda me: me ^ s
    return lambda me: (me - s) % n


def reduce_blocks(blocks, axis):
    n = blocks.shape[0]
    me = lax.axis_index(axis)
    total = lax.dynamic_index_in_dim(blocks, me, 0, keepdims=False).astype(jnp.float32)
    for s in range(1, n):
        chunk = lax.dynamic_index_in_dim(blocks, partner_of(me, s, n), 0, keepdims=False)
        total = total + lax.ppermute(chunk, axis, pairs_for(s, n)).astype(jnp.float32)
    return total


def gather_blocks(x, axis):
    n = lax.axis_size(axis)
    me = lax.axis_index(axis)
    got = [x] + [lax.ppermute(x, axis, pairs_for(s, n)) for s in range(1, n)]
    stacked = jnp.stack(got)
    if is_pow2(n):
        order = lax.iota(jnp.int32, n) ^ me
    else:
        order = (me - lax.iota(jnp.int32, n)) % n
    return jnp.take(stacked, order, axis=0)


def swap_blocks(blocks, axis):
    n = blocks.shape[0]
    if n > 16:
        return lax.all_to_all(blocks, axis, 0, 0, tiled=True)
    me = lax.axis_index(axis)
    got = [lax.dynamic_index_in_dim(blocks, me, 0, keepdims=False)]
    for s in range(1, n):
        chunk = lax.dynamic_index_in_dim(blocks, partner_of(me, s, n), 0, keepdims=False)
        got.append(lax.ppermute(chunk, axis, pairs_for(s, n)))
    stacked = jnp.stack(got)
    if is_pow2(n):
        order = lax.iota(jnp.int32, n) ^ me
    else:
        order = (me - lax.iota(jnp.int32, n)) % n
    return jnp.take(stacked, order, axis=0)


def bit_orders(n):
    bits = [1 << i for i in range(n.bit_length() - 1)]
    return [bits, bits[::-1]]


def reduce_scatter_tree(block_fn, axis, n):
    orders = bit_orders(n)
    helds = [{d: block_fn(d, h) for d in range(n)} for h in range(len(orders))]
    for stage in range(len(orders[0])):
        payloads, keeps = [], []
        for h, order in enumerate(orders):
            bit = order[stage]
            send = sorted(d for d in helds[h] if d & bit)
            keeps.append(sorted(d for d in helds[h] if not d & bit))
            payloads.append(jnp.concatenate([helds[h][d].astype(jnp.bfloat16) for d in send], axis=0))
        payloads = lax.optimization_barrier(payloads)
        for h, order in enumerate(orders):
            bit = order[stage]
            got = lax.ppermute(payloads[h], axis, [(i, i ^ bit) for i in range(n)])
            rows = helds[h][keeps[h][0]].shape[0]
            helds[h] = {
                d: helds[h][d].astype(jnp.float32) + got[i * rows:(i + 1) * rows].astype(jnp.float32)
                for i, d in enumerate(keeps[h])
            }
    return [held[0] for held in helds]


def all_gather_tree(halves, axis, n):
    orders = bit_orders(n)
    helds = [{0: halves[h]} for h in range(len(orders))]
    for stage in range(len(orders[0])):
        haves = [sorted(held) for held in helds]
        payloads = [jnp.concatenate([helds[h][d] for d in haves[h]], axis=0) for h in range(len(orders))]
        payloads = lax.optimization_barrier(payloads)
        for h, order in enumerate(orders):
            bit = order[stage]
            got = lax.ppermute(payloads[h], axis, [(i, i ^ bit) for i in range(n)])
            rows = halves[h].shape[0]
            for i, d in enumerate(haves[h]):
                helds[h][d ^ bit] = got[i * rows:(i + 1) * rows]
    return helds


def reduce_scatter_free(block_fn, axis, n):
    outs = []
    for h, order in enumerate(bit_orders(n)):
        held = {d: block_fn(d, h) for d in range(n)}
        for bit in order:
            send = sorted(d for d in held if d & bit)
            keep = sorted(d for d in held if not d & bit)
            payload = jnp.concatenate([held[d].astype(jnp.bfloat16) for d in send], axis=0)
            got = lax.ppermute(payload, axis, [(i, i ^ bit) for i in range(n)])
            rows = held[keep[0]].shape[0]
            held = {
                d: held[d].astype(jnp.float32) + got[i * rows:(i + 1) * rows].astype(jnp.float32)
                for i, d in enumerate(keep)
            }
        outs.append(held[0])
    return outs


def all_gather_free(halves, axis, n):
    outs = []
    for h, order in enumerate(bit_orders(n)):
        held = {0: halves[h]}
        for bit in order:
            have = sorted(held)
            payload = jnp.concatenate([held[d] for d in have], axis=0)
            got = lax.ppermute(payload, axis, [(i, i ^ bit) for i in range(n)])
            rows = halves[h].shape[0]
            for i, d in enumerate(have):
                held[d ^ bit] = got[i * rows:(i + 1) * rows]
        outs.append(held)
    return outs


def dispatch_rows(blocks, axis):
    n = blocks.shape[0]
    if n > 16 or not is_pow2(n):
        arrived = lax.all_to_all(blocks, axis, 0, 0, tiled=True)
        return [arrived[p] for p in range(n)]
    me = lax.axis_index(axis)
    got = [lax.dynamic_index_in_dim(blocks, me, 0, keepdims=False)]
    for s in range(1, n):
        chunk = lax.dynamic_index_in_dim(blocks, me ^ s, 0, keepdims=False)
        got.append(lax.ppermute(chunk, axis, [(i, i ^ s) for i in range(n)]))
    return got


def collect_rows(parts, axis):
    n = len(parts)
    if n > 16 or not is_pow2(n):
        return lax.all_to_all(jnp.stack(parts), axis, 0, 0, tiled=True)
    me = lax.axis_index(axis)
    got = [parts[0]] + [
        lax.ppermute(parts[s], axis, [(i, i ^ s) for i in range(n)]) for s in range(1, n)
    ]
    return jnp.take(jnp.stack(got), lax.iota(jnp.int32, n) ^ me, axis=0)


SLOT_CHUNKS = 1


def shards(context, residual_in, out_proj, members, host_group, member_proj, member_head):
    tok_rows, width = context.shape
    group_count = lax.axis_size("dp")
    tensor_count = lax.axis_size("tensor")
    capacity = max(2, (5 * tok_rows + 4 * group_count - 1) // (4 * group_count))
    chunks = SLOT_CHUNKS if capacity % SLOT_CHUNKS == 0 else 1
    chunk_cap = capacity // chunks
    chunk_slots = group_count * chunk_cap
    me_t = lax.axis_index("tensor")
    partners = [partner_of(me_t, s, tensor_count) for s in range(tensor_count)]
    projection = member_proj[0]
    proj_blocks = projection.reshape(tensor_count, width, projection.shape[1])
    proj_parts = [lax.dynamic_index_in_dim(proj_blocks, p, 0, keepdims=False) for p in partners]

    tree = is_pow2(tensor_count) and tensor_count > 1 and width % 2 == 0
    half = width // 2

    def head_term(p):
        columns = lax.dynamic_slice_in_dim(out_proj, p * width, width, axis=1)
        return jnp.dot(context, columns, preferred_element_type=jnp.float32).astype(jnp.bfloat16)

    if tree:
        head_rows = jnp.dot(context, out_proj, preferred_element_type=jnp.float32).astype(jnp.bfloat16)
        row_half = tok_rows // 2

        def head_half(d, h):
            rows = head_rows[h * row_half:(h + 1) * row_half]
            return lax.dynamic_slice_in_dim(rows, (me_t ^ d) * width, width, axis=1)

        summed = jnp.concatenate(reduce_scatter_free(head_half, "tensor", tensor_count), axis=0)
        summed = summed + residual_in.astype(jnp.float32)
    else:
        received = [
            lax.ppermute(head_term(partners[s]), "tensor", pairs_for(s, tensor_count))
            for s in range(1, tensor_count)
        ]
        summed = head_term(me_t).astype(jnp.float32) + residual_in.astype(jnp.float32)
        for got in received:
            summed = summed + got.astype(jnp.float32)
    generated = summed.astype(jnp.bfloat16)

    group_ids = lax.iota(jnp.int32, group_count)
    member_ids = members[:, 0]
    destination = jnp.sum(
        jnp.where(member_ids[:, None] == group_ids[None, :], host_group[None, :], 0), axis=1
    )
    dest_hot = (destination[:, None] == group_ids[None, :]).astype(jnp.int32)
    earlier = jnp.cumsum(dest_hot, axis=0) - dest_hot
    rank_in = jnp.sum(earlier * dest_hot, axis=1)
    slot_ids = lax.iota(jnp.int32, chunk_slots)
    head_row = member_head[0][None, :]

    if tree:
        rank_ok = rank_in < capacity
        slot_of = destination * capacity + rank_in
        placing = ((slot_of[:, None] == lax.iota(jnp.int32, group_count * capacity)[None, :])
                   & rank_ok[:, None]).astype(jnp.bfloat16)
        outgoing = lax.dot_general(
            placing, generated, (((0,), (0,)), ((), ())), preferred_element_type=jnp.float32
        ).astype(jnp.bfloat16)
        arrived = dispatch_rows(outgoing.reshape(group_count, capacity, width), "dp")
        wave = max(1, group_count // 2)
        waves = [arrived[:wave], arrived[wave:]] if group_count > 1 else [arrived]
        grads = []
        for blocks in waves:
            rows_in = jnp.concatenate(blocks, axis=0)
            held = all_gather_free([rows_in[:, :half], rows_in[:, half:]], "tensor", tensor_count)
            pre_act = None
            for h in range(2):
                for d in range(tensor_count):
                    rows_w = lax.dynamic_slice_in_dim(projection, (me_t ^ d) * width + h * half, half, axis=0)
                    term = jnp.dot(held[h][d], rows_w, preferred_element_type=jnp.float32)
                    pre_act = term if pre_act is None else pre_act + term
            pre_grad = (-slope_times(pre_act, jnp.broadcast_to(head_row, pre_act.shape))).astype(jnp.bfloat16)

            def back_half(d, h, pre_grad=pre_grad):
                rows_w = lax.dynamic_slice_in_dim(projection, (me_t ^ d) * width + h * half, half, axis=0)
                return lax.dot_general(
                    pre_grad, rows_w, (((1,), (1,)), ((), ())), preferred_element_type=jnp.float32
                ).astype(jnp.bfloat16)

            grad = jnp.concatenate(
                reduce_scatter_free(back_half, "tensor", tensor_count), axis=1
            ).astype(jnp.bfloat16)
            grads.extend(jnp.split(grad, len(blocks), axis=0))
        returned = collect_rows(grads, "dp").reshape(group_count * capacity, width)
        input_grad = jnp.dot(placing, returned, preferred_element_type=jnp.float32)
        return (generated, input_grad.astype(jnp.bfloat16))

    input_grad = None
    for c in range(chunks):
        local_rank = rank_in - c * chunk_cap
        inside = (local_rank >= 0) & (local_rank < chunk_cap)
        slot_of = destination * chunk_cap + local_rank
        placing = ((slot_of[:, None] == slot_ids[None, :]) & inside[:, None]).astype(jnp.bfloat16)
        outgoing = lax.dot_general(
            placing, generated, (((0,), (0,)), ((), ())), preferred_element_type=jnp.float32
        ).astype(jnp.bfloat16)
        arrived = swap_blocks(outgoing.reshape(group_count, chunk_cap, width), "dp")
        arrived = arrived.reshape(chunk_slots, width)
        if tree:
            pre_act = None
            held = all_gather_free([arrived[:, :half], arrived[:, half:]], "tensor", tensor_count)
            for h in range(2):
                for d in range(tensor_count):
                    rows_w = lax.dynamic_slice_in_dim(projection, (me_t ^ d) * width + h * half, half, axis=0)
                    term = jnp.dot(held[h][d], rows_w, preferred_element_type=jnp.float32)
                    pre_act = term if pre_act is None else pre_act + term
        else:
            pre_act = jnp.dot(arrived, proj_parts[0], preferred_element_type=jnp.float32)
            for s in range(1, tensor_count):
                got = lax.ppermute(arrived, "tensor", pairs_for(s, tensor_count))
                pre_act = pre_act + jnp.dot(got, proj_parts[s], preferred_element_type=jnp.float32)
        pre_grad = (-slope_times(pre_act, jnp.broadcast_to(head_row, pre_act.shape))).astype(jnp.bfloat16)
        if tree:
            def back_half(d, h):
                rows_w = lax.dynamic_slice_in_dim(projection, (me_t ^ d) * width + h * half, half, axis=0)
                return lax.dot_general(
                    pre_grad, rows_w, (((1,), (1,)), ((), ())), preferred_element_type=jnp.float32
                ).astype(jnp.bfloat16)

            critic_grad = jnp.concatenate(
                reduce_scatter_free(back_half, "tensor", tensor_count), axis=1
            ).astype(jnp.bfloat16)
        else:
            back = [
                lax.dot_general(
                    pre_grad, part, (((1,), (1,)), ((), ())), preferred_element_type=jnp.float32
                ).astype(jnp.bfloat16)
                for part in proj_parts
            ]
            critic_grad = back[0].astype(jnp.float32)
            for s in range(1, tensor_count):
                critic_grad = critic_grad + lax.ppermute(
                    back[s], "tensor", pairs_for(s, tensor_count)
                ).astype(jnp.float32)
            critic_grad = critic_grad.astype(jnp.bfloat16)
        returned = swap_blocks(critic_grad.reshape(group_count, chunk_cap, width), "dp")
        returned = returned.reshape(chunk_slots, width)
        part = jnp.dot(placing, returned, preferred_element_type=jnp.float32)
        input_grad = part if input_grad is None else input_grad + part
    return (generated, input_grad.astype(jnp.bfloat16))


def solution(mesh):
    in_specs = (
        P("dp", "tensor"),
        P("dp", "tensor"),
        P("tensor", None),
        P("dp", None),
        P(),
        P("dp", None, "tensor"),
        P("dp", "tensor"),
    )
    out_specs = (P("dp", "tensor"), P("dp", "tensor"))
    return jax.shard_map(shards, mesh=mesh, in_specs=in_specs, out_specs=out_specs, check_vma=False)
```

```python
from functools import partial

import jax
import jax.numpy as jnp
from jax import lax
from jax.sharding import PartitionSpec as P


def slope_times(values, weights):
    _, back_fn = jax.vjp(partial(jax.nn.gelu, approximate=True), values)
    return back_fn(weights)[0]


def is_pow2(n):
    return n & (n - 1) == 0


def partner_of(me, s, n):
    return me ^ s if is_pow2(n) else (me + s) % n


def pairs_for(s, n):
    if is_pow2(n):
        return [(i, i ^ s) for i in range(n)]
    return [(i, (i + s) % n) for i in range(n)]


def sources_for(s, n):
    if is_pow2(n):
        return lambda me: me ^ s
    return lambda me: (me - s) % n


def reduce_blocks(blocks, axis):
    n = blocks.shape[0]
    me = lax.axis_index(axis)
    total = lax.dynamic_index_in_dim(blocks, me, 0, keepdims=False).astype(jnp.float32)
    for s in range(1, n):
        chunk = lax.dynamic_index_in_dim(blocks, partner_of(me, s, n), 0, keepdims=False)
        total = total + lax.ppermute(chunk, axis, pairs_for(s, n)).astype(jnp.float32)
    return total


def gather_blocks(x, axis):
    n = lax.axis_size(axis)
    me = lax.axis_index(axis)
    got = [x] + [lax.ppermute(x, axis, pairs_for(s, n)) for s in range(1, n)]
    stacked = jnp.stack(got)
    if is_pow2(n):
        order = lax.iota(jnp.int32, n) ^ me
    else:
        order = (me - lax.iota(jnp.int32, n)) % n
    return jnp.take(stacked, order, axis=0)


def swap_blocks(blocks, axis):
    n = blocks.shape[0]
    if n > 16:
        return lax.all_to_all(blocks, axis, 0, 0, tiled=True)
    me = lax.axis_index(axis)
    got = [lax.dynamic_index_in_dim(blocks, me, 0, keepdims=False)]
    for s in range(1, n):
        chunk = lax.dynamic_index_in_dim(blocks, partner_of(me, s, n), 0, keepdims=False)
        got.append(lax.ppermute(chunk, axis, pairs_for(s, n)))
    stacked = jnp.stack(got)
    if is_pow2(n):
        order = lax.iota(jnp.int32, n) ^ me
    else:
        order = (me - lax.iota(jnp.int32, n)) % n
    return jnp.take(stacked, order, axis=0)


def bit_orders(n):
    bits = [1 << i for i in range(n.bit_length() - 1)]
    return [bits, bits[::-1]]


def reduce_scatter_tree(block_fn, axis, n):
    orders = bit_orders(n)
    helds = [{d: block_fn(d, h) for d in range(n)} for h in range(len(orders))]
    for stage in range(len(orders[0])):
        payloads, keeps = [], []
        for h, order in enumerate(orders):
            bit = order[stage]
            send = sorted(d for d in helds[h] if d & bit)
            keeps.append(sorted(d for d in helds[h] if not d & bit))
            payloads.append(jnp.concatenate([helds[h][d].astype(jnp.bfloat16) for d in send], axis=0))
        payloads = lax.optimization_barrier(payloads)
        for h, order in enumerate(orders):
            bit = order[stage]
            got = lax.ppermute(payloads[h], axis, [(i, i ^ bit) for i in range(n)])
            rows = helds[h][keeps[h][0]].shape[0]
            helds[h] = {
                d: helds[h][d].astype(jnp.float32) + got[i * rows:(i + 1) * rows].astype(jnp.float32)
                for i, d in enumerate(keeps[h])
            }
    return [held[0] for held in helds]


def all_gather_tree(halves, axis, n):
    orders = bit_orders(n)
    helds = [{0: halves[h]} for h in range(len(orders))]
    for stage in range(len(orders[0])):
        haves = [sorted(held) for held in helds]
        payloads = [jnp.concatenate([helds[h][d] for d in haves[h]], axis=0) for h in range(len(orders))]
        payloads = lax.optimization_barrier(payloads)
        for h, order in enumerate(orders):
            bit = order[stage]
            got = lax.ppermute(payloads[h], axis, [(i, i ^ bit) for i in range(n)])
            rows = halves[h].shape[0]
            for i, d in enumerate(haves[h]):
                helds[h][d ^ bit] = got[i * rows:(i + 1) * rows]
    return helds


def reduce_scatter_free(block_fn, axis, n):
    outs = []
    for h, order in enumerate(bit_orders(n)):
        held = {d: block_fn(d, h) for d in range(n)}
        for bit in order:
            send = sorted(d for d in held if d & bit)
            keep = sorted(d for d in held if not d & bit)
            payload = jnp.concatenate([held[d].astype(jnp.bfloat16) for d in send], axis=0)
            got = lax.ppermute(payload, axis, [(i, i ^ bit) for i in range(n)])
            rows = held[keep[0]].shape[0]
            held = {
                d: held[d].astype(jnp.float32) + got[i * rows:(i + 1) * rows].astype(jnp.float32)
                for i, d in enumerate(keep)
            }
        outs.append(held[0])
    return outs


def all_gather_free(halves, axis, n):
    outs = []
    for h, order in enumerate(bit_orders(n)):
        held = {0: halves[h]}
        for bit in order:
            have = sorted(held)
            payload = jnp.concatenate([held[d] for d in have], axis=0)
            got = lax.ppermute(payload, axis, [(i, i ^ bit) for i in range(n)])
            rows = halves[h].shape[0]
            for i, d in enumerate(have):
                held[d ^ bit] = got[i * rows:(i + 1) * rows]
        outs.append(held)
    return outs


def dispatch_rows(blocks, axis):
    n = blocks.shape[0]
    if n > 16 or not is_pow2(n):
        arrived = lax.all_to_all(blocks, axis, 0, 0, tiled=True)
        return [arrived[p] for p in range(n)]
    me = lax.axis_index(axis)
    got = [lax.dynamic_index_in_dim(blocks, me, 0, keepdims=False)]
    for s in range(1, n):
        chunk = lax.dynamic_index_in_dim(blocks, me ^ s, 0, keepdims=False)
        got.append(lax.ppermute(chunk, axis, [(i, i ^ s) for i in range(n)]))
    return got


def collect_rows(parts, axis):
    n = len(parts)
    if n > 16 or not is_pow2(n):
        return lax.all_to_all(jnp.stack(parts), axis, 0, 0, tiled=True)
    me = lax.axis_index(axis)
    got = [parts[0]] + [
        lax.ppermute(parts[s], axis, [(i, i ^ s) for i in range(n)]) for s in range(1, n)
    ]
    return jnp.take(jnp.stack(got), lax.iota(jnp.int32, n) ^ me, axis=0)


SLOT_CHUNKS = 1


def shards(context, residual_in, out_proj, members, host_group, member_proj, member_head):
    tok_rows, width = context.shape
    group_count = lax.axis_size("dp")
    tensor_count = lax.axis_size("tensor")
    capacity = max(2, (5 * tok_rows + 4 * group_count - 1) // (4 * group_count))
    chunks = SLOT_CHUNKS if capacity % SLOT_CHUNKS == 0 else 1
    chunk_cap = capacity // chunks
    chunk_slots = group_count * chunk_cap
    me_t = lax.axis_index("tensor")
    partners = [partner_of(me_t, s, tensor_count) for s in range(tensor_count)]
    projection = member_proj[0]
    proj_blocks = projection.reshape(tensor_count, width, projection.shape[1])
    proj_parts = [lax.dynamic_index_in_dim(proj_blocks, p, 0, keepdims=False) for p in partners]

    tree = is_pow2(tensor_count) and tensor_count > 1 and width % 2 == 0
    half = width // 2

    def head_term(p):
        columns = lax.dynamic_slice_in_dim(out_proj, p * width, width, axis=1)
        return jnp.dot(context, columns, preferred_element_type=jnp.float32).astype(jnp.bfloat16)

    if tree:
        head_rows = jnp.dot(context, out_proj, preferred_element_type=jnp.float32).astype(jnp.bfloat16)
        row_half = tok_rows // 2

        def head_half(d, h):
            rows = head_rows[h * row_half:(h + 1) * row_half]
            return lax.dynamic_slice_in_dim(rows, (me_t ^ d) * width, width, axis=1)

        summed = jnp.concatenate(reduce_scatter_free(head_half, "tensor", tensor_count), axis=0)
        summed = summed + residual_in.astype(jnp.float32)
    else:
        received = [
            lax.ppermute(head_term(partners[s]), "tensor", pairs_for(s, tensor_count))
            for s in range(1, tensor_count)
        ]
        summed = head_term(me_t).astype(jnp.float32) + residual_in.astype(jnp.float32)
        for got in received:
            summed = summed + got.astype(jnp.float32)
    generated = summed.astype(jnp.bfloat16)

    group_ids = lax.iota(jnp.int32, group_count)
    member_ids = members[:, 0]
    destination = jnp.sum(
        jnp.where(member_ids[:, None] == group_ids[None, :], host_group[None, :], 0), axis=1
    )
    dest_hot = (destination[:, None] == group_ids[None, :]).astype(jnp.int32)
    earlier = jnp.cumsum(dest_hot, axis=0) - dest_hot
    rank_in = jnp.sum(earlier * dest_hot, axis=1)
    slot_ids = lax.iota(jnp.int32, chunk_slots)
    head_row = member_head[0][None, :]

    if tree:
        rank_ok = rank_in < capacity
        slot_of = destination * capacity + rank_in
        placing = ((slot_of[:, None] == lax.iota(jnp.int32, group_count * capacity)[None, :])
                   & rank_ok[:, None]).astype(jnp.bfloat16)
        outgoing = lax.dot_general(
            placing, generated, (((0,), (0,)), ((), ())), preferred_element_type=jnp.float32
        ).astype(jnp.bfloat16)
        arrived = dispatch_rows(outgoing.reshape(group_count, capacity, width), "dp")
        wave = max(1, group_count // 2)
        waves = [arrived[:wave], arrived[wave:]] if group_count > 1 else [arrived]
        grads = []
        for blocks in waves:
            rows_in = jnp.concatenate(blocks, axis=0)
            held = all_gather_free([rows_in[:, :half], rows_in[:, half:]], "tensor", tensor_count)
            pre_act = None
            for d in range(tensor_count):
                rows_w = lax.dynamic_slice_in_dim(projection, (me_t ^ d) * width, width, axis=0)
                both = jnp.concatenate([held[0][d], held[1][d]], axis=1)
                term = jnp.dot(both, rows_w, preferred_element_type=jnp.float32)
                pre_act = term if pre_act is None else pre_act + term
            pre_grad = (-slope_times(pre_act, jnp.broadcast_to(head_row, pre_act.shape))).astype(jnp.bfloat16)

            back_full = [
                lax.dot_general(
                    pre_grad,
                    lax.dynamic_slice_in_dim(projection, (me_t ^ d) * width, width, axis=0),
                    (((1,), (1,)), ((), ())),
                    preferred_element_type=jnp.float32,
                ).astype(jnp.bfloat16)
                for d in range(tensor_count)
            ]

            def back_half(d, h, back_full=back_full):
                return back_full[d][:, h * half:(h + 1) * half]

            grad = jnp.concatenate(
                reduce_scatter_free(back_half, "tensor", tensor_count), axis=1
            ).astype(jnp.bfloat16)
            grads.extend(jnp.split(grad, len(blocks), axis=0))
        returned = collect_rows(grads, "dp").reshape(group_count * capacity, width)
        input_grad = jnp.dot(placing, returned, preferred_element_type=jnp.float32)
        return (generated, input_grad.astype(jnp.bfloat16))

    input_grad = None
    for c in range(chunks):
        local_rank = rank_in - c * chunk_cap
        inside = (local_rank >= 0) & (local_rank < chunk_cap)
        slot_of = destination * chunk_cap + local_rank
        placing = ((slot_of[:, None] == slot_ids[None, :]) & inside[:, None]).astype(jnp.bfloat16)
        outgoing = lax.dot_general(
            placing, generated, (((0,), (0,)), ((), ())), preferred_element_type=jnp.float32
        ).astype(jnp.bfloat16)
        arrived = swap_blocks(outgoing.reshape(group_count, chunk_cap, width), "dp")
        arrived = arrived.reshape(chunk_slots, width)
        if tree:
            pre_act = None
            held = all_gather_free([arrived[:, :half], arrived[:, half:]], "tensor", tensor_count)
            for h in range(2):
                for d in range(tensor_count):
                    rows_w = lax.dynamic_slice_in_dim(projection, (me_t ^ d) * width + h * half, half, axis=0)
                    term = jnp.dot(held[h][d], rows_w, preferred_element_type=jnp.float32)
                    pre_act = term if pre_act is None else pre_act + term
        else:
            pre_act = jnp.dot(arrived, proj_parts[0], preferred_element_type=jnp.float32)
            for s in range(1, tensor_count):
                got = lax.ppermute(arrived, "tensor", pairs_for(s, tensor_count))
                pre_act = pre_act + jnp.dot(got, proj_parts[s], preferred_element_type=jnp.float32)
        pre_grad = (-slope_times(pre_act, jnp.broadcast_to(head_row, pre_act.shape))).astype(jnp.bfloat16)
        if tree:
            def back_half(d, h):
                rows_w = lax.dynamic_slice_in_dim(projection, (me_t ^ d) * width + h * half, half, axis=0)
                return lax.dot_general(
                    pre_grad, rows_w, (((1,), (1,)), ((), ())), preferred_element_type=jnp.float32
                ).astype(jnp.bfloat16)

            critic_grad = jnp.concatenate(
                reduce_scatter_free(back_half, "tensor", tensor_count), axis=1
            ).astype(jnp.bfloat16)
        else:
            back = [
                lax.dot_general(
                    pre_grad, part, (((1,), (1,)), ((), ())), preferred_element_type=jnp.float32
                ).astype(jnp.bfloat16)
                for part in proj_parts
            ]
            critic_grad = back[0].astype(jnp.float32)
            for s in range(1, tensor_count):
                critic_grad = critic_grad + lax.ppermute(
                    back[s], "tensor", pairs_for(s, tensor_count)
                ).astype(jnp.float32)
            critic_grad = critic_grad.astype(jnp.bfloat16)
        returned = swap_blocks(critic_grad.reshape(group_count, chunk_cap, width), "dp")
        returned = returned.reshape(chunk_slots, width)
        part = jnp.dot(placing, returned, preferred_element_type=jnp.float32)
        input_grad = part if input_grad is None else input_grad + part
    return (generated, input_grad.astype(jnp.bfloat16))


def solution(mesh):
    in_specs = (
        P("dp", "tensor"),
        P("dp", "tensor"),
        P("tensor", None),
        P("dp", None),
        P(),
        P("dp", None, "tensor"),
        P("dp", "tensor"),
    )
    out_specs = (P("dp", "tensor"), P("dp", "tensor"))
    return jax.shard_map(shards, mesh=mesh, in_specs=in_specs, out_specs=out_specs, check_vma=False)
```

```python
from functools import partial

import jax
import jax.numpy as jnp
from jax import lax
from jax.sharding import PartitionSpec as P


def slope_times(values, weights):
    _, back_fn = jax.vjp(partial(jax.nn.gelu, approximate=True), values)
    return back_fn(weights)[0]


def is_pow2(n):
    return n & (n - 1) == 0


def partner_of(me, s, n):
    return me ^ s if is_pow2(n) else (me + s) % n


def pairs_for(s, n):
    if is_pow2(n):
        return [(i, i ^ s) for i in range(n)]
    return [(i, (i + s) % n) for i in range(n)]


def sources_for(s, n):
    if is_pow2(n):
        return lambda me: me ^ s
    return lambda me: (me - s) % n


def reduce_blocks(blocks, axis):
    n = blocks.shape[0]
    me = lax.axis_index(axis)
    total = lax.dynamic_index_in_dim(blocks, me, 0, keepdims=False).astype(jnp.float32)
    for s in range(1, n):
        chunk = lax.dynamic_index_in_dim(blocks, partner_of(me, s, n), 0, keepdims=False)
        total = total + lax.ppermute(chunk, axis, pairs_for(s, n)).astype(jnp.float32)
    return total


def gather_blocks(x, axis):
    n = lax.axis_size(axis)
    me = lax.axis_index(axis)
    got = [x] + [lax.ppermute(x, axis, pairs_for(s, n)) for s in range(1, n)]
    stacked = jnp.stack(got)
    if is_pow2(n):
        order = lax.iota(jnp.int32, n) ^ me
    else:
        order = (me - lax.iota(jnp.int32, n)) % n
    return jnp.take(stacked, order, axis=0)


def swap_blocks(blocks, axis):
    n = blocks.shape[0]
    if n > 16:
        return lax.all_to_all(blocks, axis, 0, 0, tiled=True)
    me = lax.axis_index(axis)
    got = [lax.dynamic_index_in_dim(blocks, me, 0, keepdims=False)]
    for s in range(1, n):
        chunk = lax.dynamic_index_in_dim(blocks, partner_of(me, s, n), 0, keepdims=False)
        got.append(lax.ppermute(chunk, axis, pairs_for(s, n)))
    stacked = jnp.stack(got)
    if is_pow2(n):
        order = lax.iota(jnp.int32, n) ^ me
    else:
        order = (me - lax.iota(jnp.int32, n)) % n
    return jnp.take(stacked, order, axis=0)


def bit_orders(n):
    bits = [1 << i for i in range(n.bit_length() - 1)]
    return [bits, bits[::-1]]


def reduce_scatter_tree(block_fn, axis, n):
    orders = bit_orders(n)
    helds = [{d: block_fn(d, h) for d in range(n)} for h in range(len(orders))]
    for stage in range(len(orders[0])):
        payloads, keeps = [], []
        for h, order in enumerate(orders):
            bit = order[stage]
            send = sorted(d for d in helds[h] if d & bit)
            keeps.append(sorted(d for d in helds[h] if not d & bit))
            payloads.append(jnp.concatenate([helds[h][d].astype(jnp.bfloat16) for d in send], axis=0))
        payloads = lax.optimization_barrier(payloads)
        for h, order in enumerate(orders):
            bit = order[stage]
            got = lax.ppermute(payloads[h], axis, [(i, i ^ bit) for i in range(n)])
            rows = helds[h][keeps[h][0]].shape[0]
            helds[h] = {
                d: helds[h][d].astype(jnp.float32) + got[i * rows:(i + 1) * rows].astype(jnp.float32)
                for i, d in enumerate(keeps[h])
            }
    return [held[0] for held in helds]


def all_gather_tree(halves, axis, n):
    orders = bit_orders(n)
    helds = [{0: halves[h]} for h in range(len(orders))]
    for stage in range(len(orders[0])):
        haves = [sorted(held) for held in helds]
        payloads = [jnp.concatenate([helds[h][d] for d in haves[h]], axis=0) for h in range(len(orders))]
        payloads = lax.optimization_barrier(payloads)
        for h, order in enumerate(orders):
            bit = order[stage]
            got = lax.ppermute(payloads[h], axis, [(i, i ^ bit) for i in range(n)])
            rows = halves[h].shape[0]
            for i, d in enumerate(haves[h]):
                helds[h][d ^ bit] = got[i * rows:(i + 1) * rows]
    return helds


def reduce_scatter_free(block_fn, axis, n):
    outs = []
    for h, order in enumerate(bit_orders(n)):
        held = {d: block_fn(d, h) for d in range(n)}
        for bit in order:
            send = sorted(d for d in held if d & bit)
            keep = sorted(d for d in held if not d & bit)
            payload = jnp.concatenate([held[d].astype(jnp.bfloat16) for d in send], axis=0)
            got = lax.ppermute(payload, axis, [(i, i ^ bit) for i in range(n)])
            rows = held[keep[0]].shape[0]
            held = {
                d: held[d].astype(jnp.float32) + got[i * rows:(i + 1) * rows].astype(jnp.float32)
                for i, d in enumerate(keep)
            }
        outs.append(held[0])
    return outs


def all_gather_free(halves, axis, n):
    outs = []
    for h, order in enumerate(bit_orders(n)):
        held = {0: halves[h]}
        for bit in order:
            have = sorted(held)
            payload = jnp.concatenate([held[d] for d in have], axis=0)
            got = lax.ppermute(payload, axis, [(i, i ^ bit) for i in range(n)])
            rows = halves[h].shape[0]
            for i, d in enumerate(have):
                held[d ^ bit] = got[i * rows:(i + 1) * rows]
        outs.append(held)
    return outs


def dispatch_rows(blocks, axis):
    n = blocks.shape[0]
    if n > 16 or not is_pow2(n):
        arrived = lax.all_to_all(blocks, axis, 0, 0, tiled=True)
        return [arrived[p] for p in range(n)]
    me = lax.axis_index(axis)
    got = [lax.dynamic_index_in_dim(blocks, me, 0, keepdims=False)]
    for s in range(1, n):
        chunk = lax.dynamic_index_in_dim(blocks, me ^ s, 0, keepdims=False)
        got.append(lax.ppermute(chunk, axis, [(i, i ^ s) for i in range(n)]))
    return got


def collect_rows(parts, axis):
    n = len(parts)
    if n > 16 or not is_pow2(n):
        return lax.all_to_all(jnp.stack(parts), axis, 0, 0, tiled=True)
    me = lax.axis_index(axis)
    got = [parts[0]] + [
        lax.ppermute(parts[s], axis, [(i, i ^ s) for i in range(n)]) for s in range(1, n)
    ]
    return jnp.take(jnp.stack(got), lax.iota(jnp.int32, n) ^ me, axis=0)


SLOT_CHUNKS = 1


def shards(context, residual_in, out_proj, members, host_group, member_proj, member_head):
    tok_rows, width = context.shape
    group_count = lax.axis_size("dp")
    tensor_count = lax.axis_size("tensor")
    capacity = max(2, (5 * tok_rows + 4 * group_count - 1) // (4 * group_count))
    chunks = SLOT_CHUNKS if capacity % SLOT_CHUNKS == 0 else 1
    chunk_cap = capacity // chunks
    chunk_slots = group_count * chunk_cap
    me_t = lax.axis_index("tensor")
    partners = [partner_of(me_t, s, tensor_count) for s in range(tensor_count)]
    projection = member_proj[0]
    proj_blocks = projection.reshape(tensor_count, width, projection.shape[1])
    proj_parts = [lax.dynamic_index_in_dim(proj_blocks, p, 0, keepdims=False) for p in partners]

    tree = is_pow2(tensor_count) and tensor_count > 1 and width % 2 == 0
    half = width // 2

    def head_term(p):
        columns = lax.dynamic_slice_in_dim(out_proj, p * width, width, axis=1)
        return jnp.dot(context, columns, preferred_element_type=jnp.float32).astype(jnp.bfloat16)

    if tree:
        head_rows = jnp.dot(context, out_proj, preferred_element_type=jnp.float32).astype(jnp.bfloat16)
        row_half = tok_rows // 2

        def head_half(d, h):
            rows = head_rows[h * row_half:(h + 1) * row_half]
            return lax.dynamic_slice_in_dim(rows, (me_t ^ d) * width, width, axis=1)

        summed = jnp.concatenate(reduce_scatter_free(head_half, "tensor", tensor_count), axis=0)
        summed = summed + residual_in.astype(jnp.float32)
    else:
        received = [
            lax.ppermute(head_term(partners[s]), "tensor", pairs_for(s, tensor_count))
            for s in range(1, tensor_count)
        ]
        summed = head_term(me_t).astype(jnp.float32) + residual_in.astype(jnp.float32)
        for got in received:
            summed = summed + got.astype(jnp.float32)
    generated = summed.astype(jnp.bfloat16)

    group_ids = lax.iota(jnp.int32, group_count)
    member_ids = members[:, 0]
    destination = jnp.sum(
        jnp.where(member_ids[:, None] == group_ids[None, :], host_group[None, :], 0), axis=1
    )
    dest_hot = (destination[:, None] == group_ids[None, :]).astype(jnp.int32)
    earlier = jnp.cumsum(dest_hot, axis=0) - dest_hot
    rank_in = jnp.sum(earlier * dest_hot, axis=1)
    slot_ids = lax.iota(jnp.int32, chunk_slots)
    head_row = member_head[0][None, :]

    if tree:
        def proj_parts_of(d):
            return lax.dynamic_slice_in_dim(projection, (me_t ^ d) * width, width, axis=0)

        rank_ok = rank_in < capacity
        slot_of = destination * capacity + rank_in
        placing = ((slot_of[:, None] == lax.iota(jnp.int32, group_count * capacity)[None, :])
                   & rank_ok[:, None]).astype(jnp.bfloat16)
        outgoing = lax.dot_general(
            placing, generated, (((0,), (0,)), ((), ())), preferred_element_type=jnp.float32
        ).astype(jnp.bfloat16)
        arrived = dispatch_rows(outgoing.reshape(group_count, capacity, width), "dp")
        wave = max(1, group_count // 2)
        waves = [arrived[:wave], arrived[wave:]] if group_count > 1 else [arrived]
        grads = []
        for blocks in waves:
            rows_in = jnp.concatenate(blocks, axis=0)
            pre_act = jnp.dot(rows_in, proj_parts_of(0), preferred_element_type=jnp.float32)
            for s in range(1, tensor_count):
                got = lax.ppermute(rows_in, "tensor", pairs_for(s, tensor_count))
                pre_act = pre_act + jnp.dot(got, proj_parts_of(s), preferred_element_type=jnp.float32)
            pre_grad = (-slope_times(pre_act, jnp.broadcast_to(head_row, pre_act.shape))).astype(jnp.bfloat16)
            back_full = [
                lax.dot_general(
                    pre_grad, proj_parts_of(d), (((1,), (1,)), ((), ())), preferred_element_type=jnp.float32
                ).astype(jnp.bfloat16)
                for d in range(tensor_count)
            ]
            grad = back_full[0].astype(jnp.float32)
            for s in range(1, tensor_count):
                grad = grad + lax.ppermute(back_full[s], "tensor", pairs_for(s, tensor_count)).astype(jnp.float32)
            grad = grad.astype(jnp.bfloat16)
            grads.extend(jnp.split(grad, len(blocks), axis=0))
        returned = collect_rows(grads, "dp").reshape(group_count * capacity, width)
        input_grad = jnp.dot(placing, returned, preferred_element_type=jnp.float32)
        return (generated, input_grad.astype(jnp.bfloat16))

    input_grad = None
    for c in range(chunks):
        local_rank = rank_in - c * chunk_cap
        inside = (local_rank >= 0) & (local_rank < chunk_cap)
        slot_of = destination * chunk_cap + local_rank
        placing = ((slot_of[:, None] == slot_ids[None, :]) & inside[:, None]).astype(jnp.bfloat16)
        outgoing = lax.dot_general(
            placing, generated, (((0,), (0,)), ((), ())), preferred_element_type=jnp.float32
        ).astype(jnp.bfloat16)
        arrived = swap_blocks(outgoing.reshape(group_count, chunk_cap, width), "dp")
        arrived = arrived.reshape(chunk_slots, width)
        if tree:
            pre_act = None
            held = all_gather_free([arrived[:, :half], arrived[:, half:]], "tensor", tensor_count)
            for h in range(2):
                for d in range(tensor_count):
                    rows_w = lax.dynamic_slice_in_dim(projection, (me_t ^ d) * width + h * half, half, axis=0)
                    term = jnp.dot(held[h][d], rows_w, preferred_element_type=jnp.float32)
                    pre_act = term if pre_act is None else pre_act + term
        else:
            pre_act = jnp.dot(arrived, proj_parts[0], preferred_element_type=jnp.float32)
            for s in range(1, tensor_count):
                got = lax.ppermute(arrived, "tensor", pairs_for(s, tensor_count))
                pre_act = pre_act + jnp.dot(got, proj_parts[s], preferred_element_type=jnp.float32)
        pre_grad = (-slope_times(pre_act, jnp.broadcast_to(head_row, pre_act.shape))).astype(jnp.bfloat16)
        if tree:
            def back_half(d, h):
                rows_w = lax.dynamic_slice_in_dim(projection, (me_t ^ d) * width + h * half, half, axis=0)
                return lax.dot_general(
                    pre_grad, rows_w, (((1,), (1,)), ((), ())), preferred_element_type=jnp.float32
                ).astype(jnp.bfloat16)

            critic_grad = jnp.concatenate(
                reduce_scatter_free(back_half, "tensor", tensor_count), axis=1
            ).astype(jnp.bfloat16)
        else:
            back = [
                lax.dot_general(
                    pre_grad, part, (((1,), (1,)), ((), ())), preferred_element_type=jnp.float32
                ).astype(jnp.bfloat16)
                for part in proj_parts
            ]
            critic_grad = back[0].astype(jnp.float32)
            for s in range(1, tensor_count):
                critic_grad = critic_grad + lax.ppermute(
                    back[s], "tensor", pairs_for(s, tensor_count)
                ).astype(jnp.float32)
            critic_grad = critic_grad.astype(jnp.bfloat16)
        returned = swap_blocks(critic_grad.reshape(group_count, chunk_cap, width), "dp")
        returned = returned.reshape(chunk_slots, width)
        part = jnp.dot(placing, returned, preferred_element_type=jnp.float32)
        input_grad = part if input_grad is None else input_grad + part
    return (generated, input_grad.astype(jnp.bfloat16))


def solution(mesh):
    in_specs = (
        P("dp", "tensor"),
        P("dp", "tensor"),
        P("tensor", None),
        P("dp", None),
        P(),
        P("dp", None, "tensor"),
        P("dp", "tensor"),
    )
    out_specs = (P("dp", "tensor"), P("dp", "tensor"))
    return jax.shard_map(shards, mesh=mesh, in_specs=in_specs, out_specs=out_specs, check_vma=False)
```
